256 devices in a mesh: dp: 8 (over z), seq: 32 (over y, x, core).
Axes of the slice: x: 4, y: 4, z: 8, core: 2. Of those that a mesh axis runs over, the one named last changes fastest.
Arguments:
- inputs: bfloat16 [8, 4096, 2048], P('dp', 'seq'), may hold values from -6 to 6
- weight_codes: bfloat16 [2048, 1280], P('seq'), may hold values from -4 to 4
- scales: bfloat16 [2048, 10], P('seq'), may hold values from 0.010986328 to 0.043945312
- log_decay: float32 [8, 16, 4096], P('dp', None, 'seq'), may hold values from -0.85 to 0, as said below
- cotangent: bfloat16 [8, 4096, 1024], P('dp', 'seq'), may hold values from -6 to 6
Outputs:
- grad_inputs: float32 [8, 4096, 2048], P('dp', 'seq')
- grad_weight: float32 [2048, 1280], P('seq')
The draws below stay inside these ranges and needn't reach their ends.
Inputs may be any that keep to these rules, and one draw needn't show every extreme that they name: log_decay is negative everywhere.
All inputs are finite; a program needn't handle non-finite values.
Results may differ from the reference program's by a relative error of at most 0.017.
Values may be sent and summed in bfloat16 or wider, within the bound.
No kernel may reach another device: no remote copies, remote signals or barrier semaphores. Data moves between devices by JAX's collectives and lax.ppermute only.
A program may use at most 128 MiB of HBM per device.

```python
import math
import jax
import jax.numpy as jnp
from jax import lax

D = 2048
HEADS = 16
HEAD_DIM = 64
QBLOCK = 128
TOTAL_STREAMS = 8
STREAM_LENGTH = 4096
PROJ = 1280


def draw_log_decay(key, part):
    random_keys = jax.random.split(key, 6)
    complete_shape = (TOTAL_STREAMS, HEADS, STREAM_LENGTH)
    head_shape = (TOTAL_STREAMS, HEADS, 1)
    fast_share = 0.5
    quick_heads = jax.random.uniform(random_keys[0], head_shape) < fast_share
    fast_rate = jnp.exp(jax.random.uniform(random_keys[1], head_shape, minval=math.log(0.045), maxval=math.log(0.075)))
    slow_rate = jnp.exp(jax.random.uniform(random_keys[2], head_shape, minval=math.log(0.05), maxval=math.log(0.2))) / STREAM_LENGTH
    baseline_rate = jnp.where(quick_heads, fast_rate, slow_rate)
    coarse_factor = jnp.exp(jax.random.uniform(random_keys[3], complete_shape, minval=-math.log(2.0), maxval=math.log(2.0)))
    spike_mask = jax.random.uniform(random_keys[4], (TOTAL_STREAMS, 1, STREAM_LENGTH)) < 3.0 / STREAM_LENGTH
    spike_loss = jax.random.uniform(random_keys[5], complete_shape, minval=math.log(0.5), maxval=math.log(0.8))
    return (-baseline_rate * coarse_factor + jnp.where(spike_mask, spike_loss, 0.0)).astype(jnp.float32)


def spiked(array, key, source, target, shards_of, factor):
    owner, partner = [(jnp.arange(array.shape[axis_at]) // (array.shape[axis_at] // shards_of)).reshape([-1 if axis == axis_at else 1 for axis in range(array.ndim)]) for axis_at in (source, target)]
    chosen = jax.random.permutation(key, shards_of)[partner]
    strong = (owner == chosen) | (owner == (partner + shards_of // 2) % shards_of)
    return jnp.where(strong, factor * array, array)


def level_of(key, extent, shards, smallest, high):
    loudness, own = 1.0, jax.random.fold_in(key, 6)
    for axis_at, blocks in shards:
        draws = jnp.exp(jax.random.uniform(jax.random.fold_in(own, axis_at), (blocks,), jnp.float32, smallest / len(shards), high / len(shards)))
        loudness = loudness * jnp.repeat(draws, extent[axis_at] // blocks).reshape([-1 if axis == axis_at else 1 for axis in range(len(extent))])
    return loudness


def bell_draw(own_key, dims, scale, bound, shards=(), kind=jnp.bfloat16):
    values = jax.random.normal(own_key, dims, jnp.float32) * scale
    if len(shards) > 0:
        values = level_of(own_key, dims, shards, -0.22, 0.18) * values
    return jnp.clip(values, min=-bound, max=bound).astype(kind)


def gaussian_with(own_key, shape, width, limit, cuts, heavy, dtype=jnp.bfloat16):
    array = width * jax.random.normal(own_key, shape, jnp.float32)
    if cuts:
        array = array * level_of(own_key, shape, cuts, -0.22, 0.18)
    return jnp.clip(spiked(array, jax.random.fold_in(own_key, 3), *heavy), -limit, limit).astype(dtype)


def setup_inputs(seed: int = 0) -> dict:
    arg_keys = jax.random.split(jax.random.key(seed), 6)
    inputs = gaussian_with(arg_keys[0], (TOTAL_STREAMS, STREAM_LENGTH, D), 1.0, 6.0, ((0, 8), (1, 32)), (1, 2, 32, 2.75))
    weight_codes = bell_draw(arg_keys[1], (D, PROJ), 1.0, 4.0, ((0, 32),))
    scales = jnp.clip(jnp.exp(math.log(0.043945312) - 1.3862944 * jax.random.uniform(arg_keys[2], (D, PROJ // QBLOCK), jnp.float32) ** level_of(arg_keys[2], (D, PROJ // QBLOCK), ((0, 32),), -0.2, 0.2)), 0.010986328, 0.043945312).astype(jnp.bfloat16)
    log_decay = draw_log_decay(jax.random.fold_in(arg_keys[5], 71), 0)
    cotangent = bell_draw(arg_keys[4], (TOTAL_STREAMS, STREAM_LENGTH, HEADS * HEAD_DIM), 1.0, 6.0, ((0, 8), (1, 32)))
    return {"inputs": inputs, "weight_codes": weight_codes, "scales": scales, "log_decay": log_decay, "cotangent": cotangent}


def dequantize(code_rows, scale_rows):
    row_count, col_count = code_rows.shape
    group_count = scale_rows.shape[1]
    spread = code_rows.astype(jnp.float32).reshape(row_count, group_count, col_count // group_count)
    spread = spread * scale_rows.astype(jnp.float32)[:, :, None]
    return spread.reshape(row_count, col_count).astype(jnp.bfloat16)

def lowered(value):
    return lax.optimization_barrier(value.astype(jnp.bfloat16)).astype(jnp.float32)

def block_prep(ld_block):
    cum_log = jnp.cumsum(ld_block, axis=1)
    input_scale = jnp.sqrt(-jnp.expm1(2.0 * ld_block))
    tail_weight = jnp.exp(cum_log[:, -1:] - cum_log) * input_scale
    return (cum_log, input_scale, tail_weight)

def weighted_pair(x_vals, grad_out, tail_weight, cum_log, inv_root):
    head_weight = jnp.exp(cum_log) * inv_root
    weighted_x = lowered(x_vals.astype(jnp.float32) * tail_weight.T[:, :, None])
    weighted_g = lowered(grad_out.astype(jnp.float32) * head_weight.T[:, :, None])
    return (weighted_x, weighted_g)

def summaries(x_vals, b_mat, c_mat, grad_out, ld_block):
    cum_log, input_scale, tail_weight = block_prep(ld_block)
    inv_root = 1.0 / math.sqrt(b_mat.shape[1])
    weighted_x, weighted_g = weighted_pair(x_vals, grad_out, tail_weight, cum_log, inv_root)
    fwd_state = jnp.einsum('sn,shp->hnp', b_mat.astype(jnp.float32), weighted_x, precision=lax.Precision.HIGHEST)
    back_state = jnp.einsum('tn,thp->hnp', c_mat.astype(jnp.float32), weighted_g, precision=lax.Precision.HIGHEST)
    return (jnp.exp(cum_log[:, -1]), fwd_state, back_state)

def block_grads(x_vals, b_mat, c_mat, grad_out, ld_block, state_in, back_in):
    block_len = ld_block.shape[1]
    cum_log, input_scale, tail_weight = block_prep(ld_block)
    inv_root = 1.0 / math.sqrt(b_mat.shape[1])
    weighted_x, weighted_g = weighted_pair(x_vals, grad_out, tail_weight, cum_log, inv_root)
    row_ids = lax.broadcasted_iota(jnp.int32, (block_len, block_len), 0)
    col_ids = lax.broadcasted_iota(jnp.int32, (block_len, block_len), 1)
    lower_mask = (row_ids >= col_ids)[None]
    log_gap = cum_log[:, :, None] - cum_log[:, None, :]
    decay_mat = jnp.where(lower_mask, jnp.exp(jnp.where(lower_mask, log_gap, 0.0)), 0.0)
    x_full = x_vals.astype(jnp.float32)
    g_full = grad_out.astype(jnp.float32)
    b_full = b_mat.astype(jnp.float32)
    c_full = c_mat.astype(jnp.float32)
    state_low = lowered(state_in)
    back_low = lowered(back_in)
    x_dot_g = jnp.einsum('thp,shp->hts', g_full, x_full, precision=lax.Precision.HIGHEST)
    c_dot_b = jnp.dot(c_full, b_full.T, precision=lax.Precision.HIGHEST)
    mix_weights = lowered(lax.optimization_barrier(jnp.sum(decay_mat * input_scale[:, None, :] * x_dot_g, axis=0)) * inv_root)
    d_c = jnp.einsum('hnp,thp->tn', state_low, weighted_g, precision=lax.Precision.HIGHEST)
    d_c = d_c + jnp.dot(mix_weights, b_full, precision=lax.Precision.HIGHEST)
    d_b = jnp.einsum('hnp,thp->tn', back_low, weighted_x, precision=lax.Precision.HIGHEST)
    d_b = d_b + jnp.dot(mix_weights.T, c_full, precision=lax.Precision.HIGHEST)
    d_x = jnp.einsum('tn,hnp->thp', b_full, back_low, precision=lax.Precision.HIGHEST) * tail_weight.T[:, :, None]
    inner_weights = lowered(decay_mat * c_dot_b[None] * inv_root)
    inner = jnp.einsum('hus,uhp->shp', inner_weights, g_full, precision=lax.Precision.HIGHEST)
    d_x = d_x + input_scale.T[:, :, None] * inner
    return (d_x, d_b, d_c)

def state_chain(decays, adds, start, backward):

    def step(carry, item):
        return (item[0][:, None, None] * carry + item[1], carry)
    return lax.scan(step, start, (decays, adds), reverse=backward)

def reference(inputs, weight_codes, scales, log_decay, cotangent):
    weights = dequantize(weight_codes, scales)
    stream_count, seq_length, model_width = inputs.shape
    flat_inputs = inputs.reshape(stream_count * seq_length, model_width)
    projected = jnp.dot(flat_inputs, weights, preferred_element_type=jnp.float32).astype(jnp.bfloat16)
    proj_width = weights.shape[1]
    head_count = log_decay.shape[1]
    hp_width = cotangent.shape[2]
    head_dim = hp_width // head_count
    state_width = (proj_width - hp_width) // 2
    block_len = min(64, seq_length)
    block_count = seq_length // block_len

    def one_stream(item):
        proj_rows, ld_rows, grad_rows = item
        x_blocks = proj_rows[:, :hp_width].reshape(block_count, block_len, head_count, head_dim)
        b_blocks = proj_rows[:, hp_width:hp_width + state_width].reshape(block_count, block_len, state_width)
        c_blocks = proj_rows[:, hp_width + state_width:].reshape(block_count, block_len, state_width)
        g_blocks = grad_rows.reshape(block_count, block_len, head_count, head_dim)
        ld_blocks = ld_rows.reshape(head_count, block_count, block_len).transpose(1, 0, 2)
        decays, fwd_states, back_states = jax.vmap(summaries)(x_blocks, b_blocks, c_blocks, g_blocks, ld_blocks)
        zero_state = jnp.zeros((head_count, state_width, head_dim), jnp.float32)
        unused_a, state_starts = state_chain(decays, fwd_states, zero_state, False)
        unused_b, back_starts = state_chain(decays, back_states, zero_state, True)
        d_x, d_b, d_c = lax.map(lambda part_item: block_grads(*part_item), (x_blocks, b_blocks, c_blocks, g_blocks, ld_blocks, state_starts, back_starts))
        return jnp.concatenate([d_x.reshape(seq_length, hp_width), d_b.reshape(seq_length, state_width), d_c.reshape(seq_length, state_width)], axis=1).astype(jnp.bfloat16)
    d_proj = lax.map(one_stream, (projected.reshape(stream_count, seq_length, proj_width), log_decay, cotangent))
    flat_d = d_proj.reshape(stream_count * seq_length, proj_width)
    grad_inputs = lax.dot_general(flat_d, weights, (((1,), (1,)), ((), ())), preferred_element_type=jnp.float32)
    grad_inputs = grad_inputs.reshape(inputs.shape)
    grad_weight = lax.dot_general(flat_inputs, flat_d, (((0,), (0,)), ((), ())), preferred_element_type=jnp.float32)
    grad_weight = grad_weight / math.sqrt(stream_count * seq_length)
    return (grad_inputs, grad_weight)
```

```python
import math

import jax
import jax.numpy as jnp
from jax import lax
from jax.sharding import PartitionSpec as P


def shifted(value, axis, step, reverse):
    count = lax.axis_size(axis)
    if reverse:
        pairs = [(place, place - step) for place in range(step, count)]
    else:
        pairs = [(place, place + step) for place in range(count - step)]
    return lax.ppermute(value, axis, pairs)


def scan_entering(decay, state, axis, reverse):
    head_count = state.shape[0]
    packed = jnp.concatenate(
        [state.reshape(head_count, -1), jnp.broadcast_to(decay[:, None], (head_count, 128))],
        axis=1,
    )
    split = packed.shape[1] - 128
    packed = shifted(packed, axis, 1, reverse)
    step = 1
    while step < lax.axis_size(axis):
        earlier = shifted(packed, axis, step, reverse)
        later_decay = packed[:, split:]
        packed = jnp.concatenate(
            [
                later_decay[:, :1] * earlier[:, :split] + packed[:, :split],
                earlier[:, split:] * later_decay,
            ],
            axis=1,
        )
        step *= 2
    return packed[:, :split].reshape(state.shape)


def dequantize(code_rows, scale_rows):
    row_count, col_count = code_rows.shape
    group_count = scale_rows.shape[1]
    spread = code_rows.astype(jnp.float32).reshape(row_count, group_count, col_count // group_count)
    spread = spread * scale_rows.astype(jnp.float32)[:, :, None]
    return spread.reshape(row_count, col_count).astype(jnp.bfloat16)


def block_prep(ld_block):
    cum_log = jnp.cumsum(ld_block, axis=1)
    input_scale = jnp.sqrt(-jnp.expm1(2.0 * ld_block))
    tail_weight = jnp.exp(cum_log[:, -1:] - cum_log) * input_scale
    return (cum_log, input_scale, tail_weight)


def weighted_pair(x_vals, grad_out, tail_weight, cum_log, inv_root):
    head_weight = jnp.exp(cum_log) * inv_root
    weighted_x = (x_vals.astype(jnp.float32) * tail_weight.T[:, :, None]).astype(jnp.bfloat16)
    weighted_g = (grad_out.astype(jnp.float32) * head_weight.T[:, :, None]).astype(jnp.bfloat16)
    return (weighted_x, weighted_g)


def summaries(x_vals, b_mat, c_mat, grad_out, ld_block):
    cum_log, input_scale, tail_weight = block_prep(ld_block)
    inv_root = 1.0 / math.sqrt(b_mat.shape[1])
    weighted_x, weighted_g = weighted_pair(x_vals, grad_out, tail_weight, cum_log, inv_root)
    fwd_state = jnp.einsum("sn,shp->hnp", b_mat, weighted_x, preferred_element_type=jnp.float32)
    back_state = jnp.einsum("tn,thp->hnp", c_mat, weighted_g, preferred_element_type=jnp.float32)
    return (jnp.exp(cum_log[:, -1]), fwd_state, back_state)


def block_grads(x_vals, b_mat, c_mat, grad_out, ld_block, state_in, back_in):
    block_len = ld_block.shape[1]
    cum_log, input_scale, tail_weight = block_prep(ld_block)
    inv_root = 1.0 / math.sqrt(b_mat.shape[1])
    weighted_x, weighted_g = weighted_pair(x_vals, grad_out, tail_weight, cum_log, inv_root)
    row_ids = lax.broadcasted_iota(jnp.int32, (block_len, block_len), 0)
    col_ids = lax.broadcasted_iota(jnp.int32, (block_len, block_len), 1)
    lower_mask = (row_ids >= col_ids)[None]
    log_gap = cum_log[:, :, None] - cum_log[:, None, :]
    decay_mat = jnp.where(lower_mask, jnp.exp(jnp.where(lower_mask, log_gap, 0.0)), 0.0)
    state_low = state_in.astype(jnp.bfloat16)
    back_low = back_in.astype(jnp.bfloat16)
    x_dot_g = jnp.einsum("thp,shp->hts", grad_out, x_vals, preferred_element_type=jnp.float32)
    c_dot_b = jnp.dot(c_mat, b_mat.T, preferred_element_type=jnp.float32)
    mix_weights = (
        jnp.sum(decay_mat * input_scale[:, None, :] * x_dot_g, axis=0) * inv_root
    ).astype(jnp.bfloat16)
    d_c = jnp.einsum("hnp,thp->tn", state_low, weighted_g, preferred_element_type=jnp.float32)
    d_c = d_c + jnp.dot(mix_weights, b_mat, preferred_element_type=jnp.float32)
    d_b = jnp.einsum("hnp,thp->tn", back_low, weighted_x, preferred_element_type=jnp.float32)
    d_b = d_b + jnp.dot(mix_weights.T, c_mat, preferred_element_type=jnp.float32)
    d_x = (
        jnp.einsum("tn,hnp->thp", b_mat, back_low, preferred_element_type=jnp.float32)
        * tail_weight.T[:, :, None]
    )
    inner_weights = (decay_mat * c_dot_b[None] * inv_root).astype(jnp.bfloat16)
    inner = jnp.einsum("hus,uhp->shp", inner_weights, grad_out, preferred_element_type=jnp.float32)
    d_x = d_x + input_scale.T[:, :, None] * inner
    return (d_x, d_b, d_c)


def state_chain(decays, adds, start, backward):

    def step(carry, item):
        return (item[0][:, None, None] * carry + item[1], carry)

    return lax.scan(step, start, (decays, adds), reverse=backward)


def local(inputs, weight_codes, scales, log_decay, cotangent):
    tok_count = inputs.shape[1]
    features = inputs[0]
    grad_out = cotangent[0]
    head_count = log_decay.shape[1]
    hp_width = grad_out.shape[1]
    head_dim = hp_width // head_count
    proj_width = weight_codes.shape[1]
    state_width = (proj_width - hp_width) // 2
    weights = lax.all_gather(dequantize(weight_codes, scales), "seq", axis=0, tiled=True)
    projected = jnp.dot(features, weights, preferred_element_type=jnp.float32).astype(jnp.bfloat16)
    block_len = min(128, tok_count)
    block_count = tok_count // block_len
    x_blocks = projected[:, :hp_width].reshape(block_count, block_len, head_count, head_dim)
    b_blocks = projected[:, hp_width : hp_width + state_width].reshape(
        block_count, block_len, state_width
    )
    c_blocks = projected[:, hp_width + state_width :].reshape(block_count, block_len, state_width)
    g_blocks = grad_out.reshape(block_count, block_len, head_count, head_dim)
    ld_blocks = log_decay[0].reshape(head_count, block_count, block_len).transpose(1, 0, 2)
    decays, fwd_states, back_states = jax.vmap(summaries)(
        x_blocks, b_blocks, c_blocks, g_blocks, ld_blocks
    )
    zero_state = jnp.zeros((head_count, state_width, head_dim), jnp.float32)
    dev_decay = jnp.prod(decays, axis=0)
    dev_fwd, unused_a = state_chain(decays, fwd_states, zero_state, False)
    dev_back, unused_b = state_chain(decays, back_states, zero_state, True)
    carried = (None, scan_entering(dev_decay, dev_fwd, "seq", False))
    returned = (None, scan_entering(dev_decay, dev_back, "seq", True))
    unused_c, state_starts = state_chain(decays, fwd_states, carried[1], False)
    unused_d, back_starts = state_chain(decays, back_states, returned[1], True)
    d_x, d_b, d_c = lax.map(
        lambda block_item: block_grads(*block_item),
        (x_blocks, b_blocks, c_blocks, g_blocks, ld_blocks, state_starts, back_starts),
    )
    d_proj = jnp.concatenate(
        [
            d_x.reshape(tok_count, hp_width),
            d_b.reshape(tok_count, state_width),
            d_c.reshape(tok_count, state_width),
        ],
        axis=1,
    ).astype(jnp.bfloat16)
    grad_in = lax.dot_general(
        d_proj, weights, (((1,), (1,)), ((), ())), preferred_element_type=jnp.float32
    )
    seq_count = lax.axis_size("seq")
    group_count = lax.axis_size("dp")
    norm_factor = 1.0 / math.sqrt(group_count * seq_count * tok_count)
    partial_grad = lax.psum_scatter(
        lax.dot_general(
            features, d_proj, (((0,), (0,)), ((), ())), preferred_element_type=jnp.float32
        ),
        "seq",
        scatter_dimension=0,
        tiled=True,
    )
    summed_grad = lax.psum(partial_grad, "dp")
    return (grad_in[None], summed_grad * norm_factor)


def solution(mesh):
    placed = (
        P("dp", "seq", None),
        P("seq", None),
        P("seq", None),
        P("dp", None, "seq"),
        P("dp", "seq", None),
    )
    return jax.shard_map(
        local,
        mesh=mesh,
        in_specs=placed,
        out_specs=(P("dp", "seq", None), P("seq", None)),
        check_vma=False,
    )
```

```python
import math

import jax
import jax.numpy as jnp
from jax import lax
from jax.sharding import PartitionSpec as P


def shifted(value, axis, step, reverse):
    count = lax.axis_size(axis)
    if reverse:
        pairs = [(place, place - step) for place in range(step, count)]
    else:
        pairs = [(place, place + step) for place in range(count - step)]
    return lax.ppermute(value.astype(jnp.bfloat16), axis, pairs).astype(value.dtype)


def scan_entering(decay, state, axis, reverse):
    head_count = state.shape[0]
    packed = jnp.concatenate(
        [state.reshape(head_count, -1), jnp.broadcast_to(decay[:, None], (head_count, 128))],
        axis=1,
    )
    split = packed.shape[1] - 128
    packed = shifted(packed, axis, 1, reverse)
    step = 1
    while step < lax.axis_size(axis):
        earlier = shifted(packed, axis, step, reverse)
        later_decay = packed[:, split:]
        packed = jnp.concatenate(
            [
                later_decay[:, :1] * earlier[:, :split] + packed[:, :split],
                earlier[:, split:] * later_decay,
            ],
            axis=1,
        )
        step *= 2
    return packed[:, :split].reshape(state.shape)


def butterfly_sum(value, axis):
    count = lax.axis_size(axis)
    step = 1
    while step < count:
        pairs = [(place, place ^ step) for place in range(count)]
        value = value + lax.ppermute(value, axis, pairs)
        step *= 2
    return value


def dequantize(code_rows, scale_rows):
    row_count, col_count = code_rows.shape
    group_count = scale_rows.shape[1]
    spread = code_rows.astype(jnp.float32).reshape(row_count, group_count, col_count // group_count)
    spread = spread * scale_rows.astype(jnp.float32)[:, :, None]
    return spread.reshape(row_count, col_count).astype(jnp.bfloat16)


def block_prep(ld_block):
    cum_log = jnp.cumsum(ld_block, axis=1)
    input_scale = jnp.sqrt(-jnp.expm1(2.0 * ld_block))
    tail_weight = jnp.exp(cum_log[:, -1:] - cum_log) * input_scale
    return (cum_log, input_scale, tail_weight)


def weighted_pair(x_vals, grad_out, tail_weight, cum_log, inv_root):
    head_weight = jnp.exp(cum_log) * inv_root
    weighted_x = (x_vals.astype(jnp.float32) * tail_weight.T[:, :, None]).astype(jnp.bfloat16)
    weighted_g = (grad_out.astype(jnp.float32) * head_weight.T[:, :, None]).astype(jnp.bfloat16)
    return (weighted_x, weighted_g)


def summaries(x_vals, b_mat, c_mat, grad_out, ld_block):
    cum_log, input_scale, tail_weight = block_prep(ld_block)
    inv_root = 1.0 / math.sqrt(b_mat.shape[1])
    weighted_x, weighted_g = weighted_pair(x_vals, grad_out, tail_weight, cum_log, inv_root)
    fwd_state = jnp.einsum("sn,shp->hnp", b_mat, weighted_x, preferred_element_type=jnp.float32)
    back_state = jnp.einsum("tn,thp->hnp", c_mat, weighted_g, preferred_element_type=jnp.float32)
    return (jnp.exp(cum_log[:, -1]), fwd_state, back_state)


def block_grads(x_vals, b_mat, c_mat, grad_out, ld_block, state_in, back_in):
    block_len = ld_block.shape[1]
    cum_log, input_scale, tail_weight = block_prep(ld_block)
    inv_root = 1.0 / math.sqrt(b_mat.shape[1])
    weighted_x, weighted_g = weighted_pair(x_vals, grad_out, tail_weight, cum_log, inv_root)
    row_ids = lax.broadcasted_iota(jnp.int32, (block_len, block_len), 0)
    col_ids = lax.broadcasted_iota(jnp.int32, (block_len, block_len), 1)
    lower_mask = (row_ids >= col_ids)[None]
    log_gap = cum_log[:, :, None] - cum_log[:, None, :]
    decay_mat = jnp.where(lower_mask, jnp.exp(jnp.where(lower_mask, log_gap, 0.0)), 0.0)
    state_low = state_in.astype(jnp.bfloat16)
    back_low = back_in.astype(jnp.bfloat16)
    x_dot_g = jnp.einsum("thp,shp->hts", grad_out, x_vals, preferred_element_type=jnp.float32)
    c_dot_b = jnp.dot(c_mat, b_mat.T, preferred_element_type=jnp.float32)
    mix_weights = (
        jnp.sum(decay_mat * input_scale[:, None, :] * x_dot_g, axis=0) * inv_root
    ).astype(jnp.bfloat16)
    d_c = jnp.einsum("hnp,thp->tn", state_low, weighted_g, preferred_element_type=jnp.float32)
    d_c = d_c + jnp.dot(mix_weights, b_mat, preferred_element_type=jnp.float32)
    d_b = jnp.einsum("hnp,thp->tn", back_low, weighted_x, preferred_element_type=jnp.float32)
    d_b = d_b + jnp.dot(mix_weights.T, c_mat, preferred_element_type=jnp.float32)
    d_x = (
        jnp.einsum("tn,hnp->thp", b_mat, back_low, preferred_element_type=jnp.float32)
        * tail_weight.T[:, :, None]
    )
    inner_weights = (decay_mat * c_dot_b[None] * inv_root).astype(jnp.bfloat16)
    inner = jnp.einsum("hus,uhp->shp", inner_weights, grad_out, preferred_element_type=jnp.float32)
    d_x = d_x + input_scale.T[:, :, None] * inner
    return (d_x, d_b, d_c)


def state_chain(decays, adds, start, backward):

    def step(carry, item):
        return (item[0][:, None, None] * carry + item[1], carry)

    return lax.scan(step, start, (decays, adds), reverse=backward)


def local(inputs, weight_codes, scales, log_decay, cotangent):
    tok_count = inputs.shape[1]
    features = inputs[0]
    grad_out = cotangent[0]
    head_count = log_decay.shape[1]
    hp_width = grad_out.shape[1]
    head_dim = hp_width // head_count
    proj_width = weight_codes.shape[1]
    state_width = (proj_width - hp_width) // 2
    weights = lax.all_gather(dequantize(weight_codes, scales), "seq", axis=0, tiled=True)
    projected = jnp.dot(features, weights, preferred_element_type=jnp.float32).astype(jnp.bfloat16)
    block_len = min(128, tok_count)
    block_count = tok_count // block_len
    x_blocks = projected[:, :hp_width].reshape(block_count, block_len, head_count, head_dim)
    b_blocks = projected[:, hp_width : hp_width + state_width].reshape(
        block_count, block_len, state_width
    )
    c_blocks = projected[:, hp_width + state_width :].reshape(block_count, block_len, state_width)
    g_blocks = grad_out.reshape(block_count, block_len, head_count, head_dim)
    ld_blocks = log_decay[0].reshape(head_count, block_count, block_len).transpose(1, 0, 2)
    decays, fwd_states, back_states = jax.vmap(summaries)(
        x_blocks, b_blocks, c_blocks, g_blocks, ld_blocks
    )
    zero_state = jnp.zeros((head_count, state_width, head_dim), jnp.float32)
    dev_decay = jnp.prod(decays, axis=0)
    dev_fwd, unused_a = state_chain(decays, fwd_states, zero_state, False)
    dev_back, unused_b = state_chain(decays, back_states, zero_state, True)
    carried = (None, scan_entering(dev_decay, dev_fwd, "seq", False))
    returned = (None, scan_entering(dev_decay, dev_back, "seq", True))
    unused_c, state_starts = state_chain(decays, fwd_states, carried[1], False)
    unused_d, back_starts = state_chain(decays, back_states, returned[1], True)
    d_x, d_b, d_c = lax.map(
        lambda block_item: block_grads(*block_item),
        (x_blocks, b_blocks, c_blocks, g_blocks, ld_blocks, state_starts, back_starts),
    )
    d_proj = jnp.concatenate(
        [
            d_x.reshape(tok_count, hp_width),
            d_b.reshape(tok_count, state_width),
            d_c.reshape(tok_count, state_width),
        ],
        axis=1,
    ).astype(jnp.bfloat16)
    grad_in = lax.dot_general(
        d_proj, weights, (((1,), (1,)), ((), ())), preferred_element_type=jnp.float32
    )
    seq_count = lax.axis_size("seq")
    group_count = lax.axis_size("dp")
    norm_factor = 1.0 / math.sqrt(group_count * seq_count * tok_count)
    partial_grad = lax.psum_scatter(
        lax.dot_general(
            features, d_proj, (((0,), (0,)), ((), ())), preferred_element_type=jnp.float32
        ),
        "seq",
        scatter_dimension=0,
        tiled=True,
    )
    summed_grad = butterfly_sum(partial_grad, "dp")
    return (grad_in[None], summed_grad * norm_factor)


def solution(mesh):
    placed = (
        P("dp", "seq", None),
        P("seq", None),
        P("seq", None),
        P("dp", None, "seq"),
        P("dp", "seq", None),
    )
    return jax.shard_map(
        local,
        mesh=mesh,
        in_specs=placed,
        out_specs=(P("dp", "seq", None), P("seq", None)),
        check_vma=False,
    )
```

```python
import math

import jax
import jax.numpy as jnp
from jax import lax
from jax.sharding import PartitionSpec as P


def shifted(value, axis, step, reverse):
    count = lax.axis_size(axis)
    if reverse:
        pairs = [(place, place - step) for place in range(step, count)]
    else:
        pairs = [(place, place + step) for place in range(count - step)]
    return lax.ppermute(value.astype(jnp.bfloat16), axis, pairs).astype(value.dtype)


def scan_entering(decay, state, axis, reverse):
    head_count = state.shape[0]
    flat = state.reshape(head_count, -1)
    split = flat.shape[1]

    def send(flat, decay, step):
        high = lax.reduce_precision(decay, exponent_bits=8, mantissa_bits=7)
        lanes = lambda part: jnp.broadcast_to(part[:, None], (head_count, 128))
        packed = jnp.concatenate([flat, lanes(high), lanes(decay - high)], axis=1)
        got = shifted(packed, axis, step, reverse)
        return got[:, :split], got[:, split] + got[:, split + 128]

    flat, decay = send(flat, decay, 1)
    step = 1
    while step < lax.axis_size(axis):
        earlier_flat, earlier_decay = send(flat, decay, step)
        flat = decay[:, None] * earlier_flat + flat
        decay = earlier_decay * decay
        step *= 2
    return flat.reshape(state.shape)


def butterfly_sum(value, axis):
    count = lax.axis_size(axis)
    step = 1
    while step < count:
        pairs = [(place, place ^ step) for place in range(count)]
        value = value + lax.ppermute(value, axis, pairs)
        step *= 2
    return value


def dequantize(code_rows, scale_rows):
    row_count, col_count = code_rows.shape
    group_count = scale_rows.shape[1]
    spread = code_rows.astype(jnp.float32).reshape(row_count, group_count, col_count // group_count)
    spread = spread * scale_rows.astype(jnp.float32)[:, :, None]
    return spread.reshape(row_count, col_count).astype(jnp.bfloat16)


def block_prep(ld_block):
    cum_log = jnp.cumsum(ld_block, axis=1)
    input_scale = jnp.sqrt(-jnp.expm1(2.0 * ld_block))
    tail_weight = jnp.exp(cum_log[:, -1:] - cum_log) * input_scale
    return (cum_log, input_scale, tail_weight)


def weighted_pair(x_vals, grad_out, tail_weight, cum_log, inv_root):
    head_weight = jnp.exp(cum_log) * inv_root
    weighted_x = (x_vals.astype(jnp.float32) * tail_weight.T[:, :, None]).astype(jnp.bfloat16)
    weighted_g = (grad_out.astype(jnp.float32) * head_weight.T[:, :, None]).astype(jnp.bfloat16)
    return (weighted_x, weighted_g)


def summaries(x_vals, b_mat, c_mat, grad_out, ld_block):
    cum_log, input_scale, tail_weight = block_prep(ld_block)
    inv_root = 1.0 / math.sqrt(b_mat.shape[1])
    weighted_x, weighted_g = weighted_pair(x_vals, grad_out, tail_weight, cum_log, inv_root)
    fwd_state = jnp.einsum("sn,shp->hnp", b_mat, weighted_x, preferred_element_type=jnp.float32)
    back_state = jnp.einsum("tn,thp->hnp", c_mat, weighted_g, preferred_element_type=jnp.float32)
    return (jnp.exp(cum_log[:, -1]), fwd_state, back_state)


def block_grads(x_vals, b_mat, c_mat, grad_out, ld_block, state_in, back_in):
    block_len = ld_block.shape[1]
    cum_log, input_scale, tail_weight = block_prep(ld_block)
    inv_root = 1.0 / math.sqrt(b_mat.shape[1])
    weighted_x, weighted_g = weighted_pair(x_vals, grad_out, tail_weight, cum_log, inv_root)
    row_ids = lax.broadcasted_iota(jnp.int32, (block_len, block_len), 0)
    col_ids = lax.broadcasted_iota(jnp.int32, (block_len, block_len), 1)
    lower_mask = (row_ids >= col_ids)[None]
    log_gap = cum_log[:, :, None] - cum_log[:, None, :]
    decay_mat = jnp.where(lower_mask, jnp.exp(jnp.where(lower_mask, log_gap, 0.0)), 0.0)
    state_low = state_in.astype(jnp.bfloat16)
    back_low = back_in.astype(jnp.bfloat16)
    x_dot_g = jnp.einsum("thp,shp->hts", grad_out, x_vals, preferred_element_type=jnp.float32)
    c_dot_b = jnp.dot(c_mat, b_mat.T, preferred_element_type=jnp.float32)
    mix_weights = (
        jnp.sum(decay_mat * input_scale[:, None, :] * x_dot_g, axis=0) * inv_root
    ).astype(jnp.bfloat16)
    d_c = jnp.einsum("hnp,thp->tn", state_low, weighted_g, preferred_element_type=jnp.float32)
    d_c = d_c + jnp.dot(mix_weights, b_mat, preferred_element_type=jnp.float32)
    d_b = jnp.einsum("hnp,thp->tn", back_low, weighted_x, preferred_element_type=jnp.float32)
    d_b = d_b + jnp.dot(mix_weights.T, c_mat, preferred_element_type=jnp.float32)
    d_x = (
        jnp.einsum("tn,hnp->thp", b_mat, back_low, preferred_element_type=jnp.float32)
        * tail_weight.T[:, :, None]
    )
    inner_weights = (decay_mat * c_dot_b[None] * inv_root).astype(jnp.bfloat16)
    inner = jnp.einsum("hus,uhp->shp", inner_weights, grad_out, preferred_element_type=jnp.float32)
    d_x = d_x + input_scale.T[:, :, None] * inner
    return (d_x, d_b, d_c)


def state_chain(decays, adds, start, backward):

    def step(carry, item):
        return (item[0][:, None, None] * carry + item[1], carry)

    return lax.scan(step, start, (decays, adds), reverse=backward)


def local(inputs, weight_codes, scales, log_decay, cotangent):
    tok_count = inputs.shape[1]
    features = inputs[0]
    grad_out = cotangent[0]
    head_count = log_decay.shape[1]
    hp_width = grad_out.shape[1]
    head_dim = hp_width // head_count
    proj_width = weight_codes.shape[1]
    state_width = (proj_width - hp_width) // 2
    weights = lax.all_gather(dequantize(weight_codes, scales), "seq", axis=0, tiled=True)
    projected = jnp.dot(features, weights, preferred_element_type=jnp.float32).astype(jnp.bfloat16)
    block_len = min(128, tok_count)
    block_count = tok_count // block_len
    x_blocks = projected[:, :hp_width].reshape(block_count, block_len, head_count, head_dim)
    b_blocks = projected[:, hp_width : hp_width + state_width].reshape(
        block_count, block_len, state_width
    )
    c_blocks = projected[:, hp_width + state_width :].reshape(block_count, block_len, state_width)
    g_blocks = grad_out.reshape(block_count, block_len, head_count, head_dim)
    ld_blocks = log_decay[0].reshape(head_count, block_count, block_len).transpose(1, 0, 2)
    decays, fwd_states, back_states = jax.vmap(summaries)(
        x_blocks, b_blocks, c_blocks, g_blocks, ld_blocks
    )
    zero_state = jnp.zeros((head_count, state_width, head_dim), jnp.float32)
    dev_decay = jnp.prod(decays, axis=0)
    dev_fwd, unused_a = state_chain(decays, fwd_states, zero_state, False)
    dev_back, unused_b = state_chain(decays, back_states, zero_state, True)
    carried = (None, scan_entering(dev_decay, dev_fwd, "seq", False))
    returned = (None, scan_entering(dev_decay, dev_back, "seq", True))
    unused_c, state_starts = state_chain(decays, fwd_states, carried[1], False)
    unused_d, back_starts = state_chain(decays, back_states, returned[1], True)
    d_x, d_b, d_c = lax.map(
        lambda block_item: block_grads(*block_item),
        (x_blocks, b_blocks, c_blocks, g_blocks, ld_blocks, state_starts, back_starts),
    )
    d_proj = jnp.concatenate(
        [
            d_x.reshape(tok_count, hp_width),
            d_b.reshape(tok_count, state_width),
            d_c.reshape(tok_count, state_width),
        ],
        axis=1,
    ).astype(jnp.bfloat16)
    grad_in = lax.dot_general(
        d_proj, weights, (((1,), (1,)), ((), ())), preferred_element_type=jnp.float32
    )
    seq_count = lax.axis_size("seq")
    group_count = lax.axis_size("dp")
    norm_factor = 1.0 / math.sqrt(group_count * seq_count * tok_count)
    partial_grad = lax.psum_scatter(
        lax.dot_general(
            features, d_proj, (((0,), (0,)), ((), ())), preferred_element_type=jnp.float32
        ).astype(jnp.bfloat16),
        "seq",
        scatter_dimension=0,
        tiled=True,
    ).astype(jnp.float32)
    summed_grad = butterfly_sum(partial_grad, "dp")
    return (grad_in[None], summed_grad * norm_factor)


def solution(mesh):
    placed = (
        P("dp", "seq", None),
        P("seq", None),
        P("seq", None),
        P("dp", None, "seq"),
        P("dp", "seq", None),
    )
    return jax.shard_map(
        local,
        mesh=mesh,
        in_specs=placed,
        out_specs=(P("dp", "seq", None), P("seq", None)),
        check_vma=False,
    )
```

```python
import math

import jax
import jax.numpy as jnp
from jax import lax
from jax.sharding import PartitionSpec as P


def shifted(value, axis, step, reverse):
    count = lax.axis_size(axis)
    if reverse:
        pairs = [(place, place - step) for place in range(step, count)]
    else:
        pairs = [(place, place + step) for place in range(count - step)]
    return lax.ppermute(value.astype(jnp.bfloat16), axis, pairs).astype(value.dtype)


def scan_entering(decay, state, axis, reverse):
    head_count = state.shape[0]
    flat = state.reshape(head_count, -1)
    split = flat.shape[1]

    def send(flat, decay, step):
        high = lax.reduce_precision(decay, exponent_bits=8, mantissa_bits=7)
        lanes = lambda part: jnp.broadcast_to(part[:, None], (head_count, 128))
        packed = jnp.concatenate([flat, lanes(high), lanes(decay - high)], axis=1)
        got = shifted(packed, axis, step, reverse)
        return got[:, :split], got[:, split] + got[:, split + 128]

    flat, decay = send(flat, decay, 1)
    step = 1
    while step < lax.axis_size(axis):
        earlier_flat, earlier_decay = send(flat, decay, step)
        flat = decay[:, None] * earlier_flat + flat
        decay = earlier_decay * decay
        step *= 2
    return flat.reshape(state.shape)


def butterfly_sum(value, axis):
    count = lax.axis_size(axis)
    step = 1
    while step < count:
        pairs = [(place, place ^ step) for place in range(count)]
        value = value + lax.ppermute(value, axis, pairs)
        step *= 2
    return value


def digit_reduce(value, axis, where, stride, radix):
    count = lax.axis_size(axis)
    digit = (lax.axis_index(axis) // stride) % radix
    total = lax.dynamic_index_in_dim(value, digit, where, False)
    for offset in range(1, radix):
        piece = lax.dynamic_index_in_dim(value, (digit + offset) % radix, where, False)
        pairs = [
            (place, place + (((place // stride) % radix + offset) % radix - (place // stride) % radix) * stride)
            for place in range(count)
        ]
        got = lax.ppermute(piece.astype(jnp.bfloat16), axis, pairs)
        total = total + got.astype(jnp.float32)
    return total


def seq_reduce_scatter(partial, axis):
    rows, cols = partial.shape
    count = lax.axis_size(axis)
    block = rows // count
    value = partial.reshape(count // 8, 4, 2, block, cols)
    value = digit_reduce(value, axis, 2, 1, 2)
    half = cols // 2
    first = digit_reduce(value[..., :half], axis, 1, 2, 4)
    first = digit_reduce(first, axis, 0, 8, count // 8)
    second = digit_reduce(value[..., half:], axis, 0, 8, count // 8)
    second = digit_reduce(second, axis, 0, 2, 4)
    return jnp.concatenate([first, second], axis=1)


def replicated_sum(value, axis):
    count = lax.axis_size(axis)
    me = lax.axis_index(axis)
    slabs = value.reshape(count, value.shape[0] // count, value.shape[1])
    total = lax.dynamic_index_in_dim(slabs, me, 0, False)
    for offset in range(1, count):
        piece = lax.dynamic_index_in_dim(slabs, (me + offset) % count, 0, False)
        pairs = [(place, (place + offset) % count) for place in range(count)]
        total = total + lax.ppermute(piece, axis, pairs)
    gathered = [total]
    for offset in range(1, count):
        pairs = [(place, (place + offset) % count) for place in range(count)]
        gathered.append(lax.ppermute(total, axis, pairs))
    stacked = jnp.stack(gathered)
    order = (me - jnp.arange(count)) % count
    return jnp.take(stacked, order, axis=0).reshape(value.shape)


def dequantize(code_rows, scale_rows):
    row_count, col_count = code_rows.shape
    group_count = scale_rows.shape[1]
    spread = code_rows.astype(jnp.float32).reshape(row_count, group_count, col_count // group_count)
    spread = spread * scale_rows.astype(jnp.float32)[:, :, None]
    return spread.reshape(row_count, col_count).astype(jnp.bfloat16)


def block_prep(ld_block):
    cum_log = jnp.cumsum(ld_block, axis=1)
    input_scale = jnp.sqrt(-jnp.expm1(2.0 * ld_block))
    tail_weight = jnp.exp(cum_log[:, -1:] - cum_log) * input_scale
    return (cum_log, input_scale, tail_weight)


def weighted_pair(x_vals, grad_out, tail_weight, cum_log, inv_root):
    head_weight = jnp.exp(cum_log) * inv_root
    weighted_x = (x_vals.astype(jnp.float32) * tail_weight.T[:, :, None]).astype(jnp.bfloat16)
    weighted_g = (grad_out.astype(jnp.float32) * head_weight.T[:, :, None]).astype(jnp.bfloat16)
    return (weighted_x, weighted_g)


def summaries(x_vals, b_mat, c_mat, grad_out, ld_block):
    cum_log, input_scale, tail_weight = block_prep(ld_block)
    inv_root = 1.0 / math.sqrt(b_mat.shape[1])
    weighted_x, weighted_g = weighted_pair(x_vals, grad_out, tail_weight, cum_log, inv_root)
    fwd_state = jnp.einsum("sn,shp->hnp", b_mat, weighted_x, preferred_element_type=jnp.float32)
    back_state = jnp.einsum("tn,thp->hnp", c_mat, weighted_g, preferred_element_type=jnp.float32)
    return (jnp.exp(cum_log[:, -1]), fwd_state, back_state)


def block_grads(x_vals, b_mat, c_mat, grad_out, ld_block, state_in, back_in):
    block_len = ld_block.shape[1]
    cum_log, input_scale, tail_weight = block_prep(ld_block)
    inv_root = 1.0 / math.sqrt(b_mat.shape[1])
    weighted_x, weighted_g = weighted_pair(x_vals, grad_out, tail_weight, cum_log, inv_root)
    row_ids = lax.broadcasted_iota(jnp.int32, (block_len, block_len), 0)
    col_ids = lax.broadcasted_iota(jnp.int32, (block_len, block_len), 1)
    lower_mask = (row_ids >= col_ids)[None]
    log_gap = cum_log[:, :, None] - cum_log[:, None, :]
    decay_mat = jnp.where(lower_mask, jnp.exp(jnp.where(lower_mask, log_gap, 0.0)), 0.0)
    state_low = state_in.astype(jnp.bfloat16)
    back_low = back_in.astype(jnp.bfloat16)
    x_dot_g = jnp.einsum("thp,shp->hts", grad_out, x_vals, preferred_element_type=jnp.float32)
    c_dot_b = jnp.dot(c_mat, b_mat.T, preferred_element_type=jnp.float32)
    mix_weights = (
        jnp.sum(decay_mat * input_scale[:, None, :] * x_dot_g, axis=0) * inv_root
    ).astype(jnp.bfloat16)
    d_c = jnp.einsum("hnp,thp->tn", state_low, weighted_g, preferred_element_type=jnp.float32)
    d_c = d_c + jnp.dot(mix_weights, b_mat, preferred_element_type=jnp.float32)
    d_b = jnp.einsum("hnp,thp->tn", back_low, weighted_x, preferred_element_type=jnp.float32)
    d_b = d_b + jnp.dot(mix_weights.T, c_mat, preferred_element_type=jnp.float32)
    d_x = (
        jnp.einsum("tn,hnp->thp", b_mat, back_low, preferred_element_type=jnp.float32)
        * tail_weight.T[:, :, None]
    )
    inner_weights = (decay_mat * c_dot_b[None] * inv_root).astype(jnp.bfloat16)
    inner = jnp.einsum("hus,uhp->shp", inner_weights, grad_out, preferred_element_type=jnp.float32)
    d_x = d_x + input_scale.T[:, :, None] * inner
    return (d_x, d_b, d_c)


def state_chain(decays, adds, start, backward):

    def step(carry, item):
        return (item[0][:, None, None] * carry + item[1], carry)

    return lax.scan(step, start, (decays, adds), reverse=backward)


def local(inputs, weight_codes, scales, log_decay, cotangent):
    tok_count = inputs.shape[1]
    features = inputs[0]
    grad_out = cotangent[0]
    head_count = log_decay.shape[1]
    hp_width = grad_out.shape[1]
    head_dim = hp_width // head_count
    proj_width = weight_codes.shape[1]
    state_width = (proj_width - hp_width) // 2
    weights = lax.all_gather(dequantize(weight_codes, scales), "seq", axis=0, tiled=True)
    projected = jnp.dot(features, weights, preferred_element_type=jnp.float32).astype(jnp.bfloat16)
    block_len = min(128, tok_count)
    block_count = tok_count // block_len
    x_blocks = projected[:, :hp_width].reshape(block_count, block_len, head_count, head_dim)
    b_blocks = projected[:, hp_width : hp_width + state_width].reshape(
        block_count, block_len, state_width
    )
    c_blocks = projected[:, hp_width + state_width :].reshape(block_count, block_len, state_width)
    g_blocks = grad_out.reshape(block_count, block_len, head_count, head_dim)
    ld_blocks = log_decay[0].reshape(head_count, block_count, block_len).transpose(1, 0, 2)
    decays, fwd_states, back_states = jax.vmap(summaries)(
        x_blocks, b_blocks, c_blocks, g_blocks, ld_blocks
    )
    zero_state = jnp.zeros((head_count, state_width, head_dim), jnp.float32)
    dev_decay = jnp.prod(decays, axis=0)
    dev_fwd, unused_a = state_chain(decays, fwd_states, zero_state, False)
    dev_back, unused_b = state_chain(decays, back_states, zero_state, True)
    carried = (None, scan_entering(dev_decay, dev_fwd, "seq", False))
    returned = (None, scan_entering(dev_decay, dev_back, "seq", True))
    unused_c, state_starts = state_chain(decays, fwd_states, carried[1], False)
    unused_d, back_starts = state_chain(decays, back_states, returned[1], True)
    d_x, d_b, d_c = lax.map(
        lambda block_item: block_grads(*block_item),
        (x_blocks, b_blocks, c_blocks, g_blocks, ld_blocks, state_starts, back_starts),
    )
    d_proj = jnp.concatenate(
        [
            d_x.reshape(tok_count, hp_width),
            d_b.reshape(tok_count, state_width),
            d_c.reshape(tok_count, state_width),
        ],
        axis=1,
    ).astype(jnp.bfloat16)
    grad_in = lax.dot_general(
        d_proj, weights, (((1,), (1,)), ((), ())), preferred_element_type=jnp.float32
    )
    seq_count = lax.axis_size("seq")
    group_count = lax.axis_size("dp")
    norm_factor = 1.0 / math.sqrt(group_count * seq_count * tok_count)
    partial_grad = seq_reduce_scatter(
        lax.dot_general(
            features, d_proj, (((0,), (0,)), ((), ())), preferred_element_type=jnp.float32
        ),
        "seq",
    )
    summed_grad = replicated_sum(partial_grad, "dp")
    return (grad_in[None], summed_grad * norm_factor)


def solution(mesh):
    placed = (
        P("dp", "seq", None),
        P("seq", None),
        P("seq", None),
        P("dp", None, "seq"),
        P("dp", "seq", None),
    )
    return jax.shard_map(
        local,
        mesh=mesh,
        in_specs=placed,
        out_specs=(P("dp", "seq", None), P("seq", None)),
        check_vma=False,
    )
```

```python
import math

import jax
import jax.numpy as jnp
from jax import lax
from jax.sharding import PartitionSpec as P


def shifted(value, axis, step, reverse):
    count = lax.axis_size(axis)
    if reverse:
        pairs = [(place, place - step) for place in range(step, count)]
    else:
        pairs = [(place, place + step) for place in range(count - step)]
    return lax.ppermute(value.astype(jnp.bfloat16), axis, pairs).astype(value.dtype)


def scan_entering(decay, state, axis, reverse):
    head_count = state.shape[0]
    flat = state.reshape(head_count, -1)
    split = flat.shape[1]

    def send(flat, decay, step):
        high = lax.reduce_precision(decay, exponent_bits=8, mantissa_bits=7)
        lanes = lambda part: jnp.broadcast_to(part[:, None], (head_count, 128))
        packed = jnp.concatenate([flat, lanes(high), lanes(decay - high)], axis=1)
        got = shifted(packed, axis, step, reverse)
        return got[:, :split], got[:, split] + got[:, split + 128]

    nearer_flat, nearer_decay = send(flat, decay, 1)
    farther_flat, farther_decay = send(flat, decay, 2)
    flat = nearer_decay[:, None] * farther_flat + nearer_flat
    decay = farther_decay * nearer_decay
    step = 2
    while step < lax.axis_size(axis):
        earlier_flat, earlier_decay = send(flat, decay, step)
        flat = decay[:, None] * earlier_flat + flat
        decay = earlier_decay * decay
        step *= 2
    return flat.reshape(state.shape)


def butterfly_sum(value, axis):
    count = lax.axis_size(axis)
    step = 1
    while step < count:
        pairs = [(place, place ^ step) for place in range(count)]
        value = value + lax.ppermute(value, axis, pairs)
        step *= 2
    return value


def digit_reduce(value, axis, where, stride, radix):
    count = lax.axis_size(axis)
    digit = (lax.axis_index(axis) // stride) % radix
    total = lax.dynamic_index_in_dim(value, digit, where, False).astype(jnp.float32)
    for offset in range(1, radix):
        piece = lax.dynamic_index_in_dim(value, (digit + offset) % radix, where, False)
        pairs = [
            (place, place + (((place // stride) % radix + offset) % radix - (place // stride) % radix) * stride)
            for place in range(count)
        ]
        got = lax.ppermute(piece.astype(jnp.bfloat16), axis, pairs)
        total = total + got.astype(jnp.float32)
    return total


def seq_reduce_scatter(partial, axis):
    rows, cols = partial.shape
    count = lax.axis_size(axis)
    block = rows // count
    value = partial.reshape(count // 8, 4, 2, block, cols)
    value = digit_reduce(value, axis, 2, 1, 2)
    half = cols // 2
    first = digit_reduce(value[..., :half], axis, 1, 2, 4)
    first = digit_reduce(first, axis, 0, 8, count // 8)
    second = digit_reduce(value[..., half:], axis, 0, 8, count // 8)
    second = digit_reduce(second, axis, 0, 2, 4)
    return jnp.concatenate([first, second], axis=1)


def replicated_sum(value, axis):
    count = lax.axis_size(axis)
    me = lax.axis_index(axis)
    slabs = value.reshape(count, value.shape[0] // count, value.shape[1])
    total = lax.dynamic_index_in_dim(slabs, me, 0, False)
    for offset in range(1, count):
        piece = lax.dynamic_index_in_dim(slabs, (me + offset) % count, 0, False)
        pairs = [(place, (place + offset) % count) for place in range(count)]
        total = total + lax.ppermute(piece, axis, pairs)
    gathered = [total]
    for offset in range(1, count):
        pairs = [(place, (place + offset) % count) for place in range(count)]
        gathered.append(lax.ppermute(total, axis, pairs))
    stacked = jnp.stack(gathered)
    order = (me - jnp.arange(count)) % count
    return jnp.take(stacked, order, axis=0).reshape(value.shape)


def dequantize(code_rows, scale_rows):
    row_count, col_count = code_rows.shape
    group_count = scale_rows.shape[1]
    spread = code_rows.astype(jnp.float32).reshape(row_count, group_count, col_count // group_count)
    spread = spread * scale_rows.astype(jnp.float32)[:, :, None]
    return spread.reshape(row_count, col_count).astype(jnp.bfloat16)


def block_prep(ld_block):
    cum_log = jnp.cumsum(ld_block, axis=1)
    input_scale = jnp.sqrt(-jnp.expm1(2.0 * ld_block))
    tail_weight = jnp.exp(cum_log[:, -1:] - cum_log) * input_scale
    return (cum_log, input_scale, tail_weight)


def weighted_pair(x_vals, grad_out, tail_weight, cum_log, inv_root):
    head_weight = jnp.exp(cum_log) * inv_root
    weighted_x = (x_vals.astype(jnp.float32) * tail_weight.T[:, :, None]).astype(jnp.bfloat16)
    weighted_g = (grad_out.astype(jnp.float32) * head_weight.T[:, :, None]).astype(jnp.bfloat16)
    return (weighted_x, weighted_g)


def summaries(x_vals, b_mat, c_mat, grad_out, ld_block):
    cum_log, input_scale, tail_weight = block_prep(ld_block)
    inv_root = 1.0 / math.sqrt(b_mat.shape[1])
    weighted_x, weighted_g = weighted_pair(x_vals, grad_out, tail_weight, cum_log, inv_root)
    fwd_state = jnp.einsum("sn,shp->hnp", b_mat, weighted_x, preferred_element_type=jnp.float32)
    back_state = jnp.einsum("tn,thp->hnp", c_mat, weighted_g, preferred_element_type=jnp.float32)
    return (jnp.exp(cum_log[:, -1]), fwd_state, back_state)


def block_grads(x_vals, b_mat, c_mat, grad_out, ld_block, state_in, back_in):
    block_len = ld_block.shape[1]
    cum_log, input_scale, tail_weight = block_prep(ld_block)
    inv_root = 1.0 / math.sqrt(b_mat.shape[1])
    weighted_x, weighted_g = weighted_pair(x_vals, grad_out, tail_weight, cum_log, inv_root)
    row_ids = lax.broadcasted_iota(jnp.int32, (block_len, block_len), 0)
    col_ids = lax.broadcasted_iota(jnp.int32, (block_len, block_len), 1)
    lower_mask = (row_ids >= col_ids)[None]
    log_gap = cum_log[:, :, None] - cum_log[:, None, :]
    decay_mat = jnp.where(lower_mask, jnp.exp(jnp.where(lower_mask, log_gap, 0.0)), 0.0)
    state_low = state_in.astype(jnp.bfloat16)
    back_low = back_in.astype(jnp.bfloat16)
    x_dot_g = jnp.einsum("thp,shp->hts", grad_out, x_vals, preferred_element_type=jnp.float32)
    c_dot_b = jnp.dot(c_mat, b_mat.T, preferred_element_type=jnp.float32)
    mix_weights = (
        jnp.sum(decay_mat * input_scale[:, None, :] * x_dot_g, axis=0) * inv_root
    ).astype(jnp.bfloat16)
    d_c = jnp.einsum("hnp,thp->tn", state_low, weighted_g, preferred_element_type=jnp.float32)
    d_c = d_c + jnp.dot(mix_weights, b_mat, preferred_element_type=jnp.float32)
    d_b = jnp.einsum("hnp,thp->tn", back_low, weighted_x, preferred_element_type=jnp.float32)
    d_b = d_b + jnp.dot(mix_weights.T, c_mat, preferred_element_type=jnp.float32)
    d_x = (
        jnp.einsum("tn,hnp->thp", b_mat, back_low, preferred_element_type=jnp.float32)
        * tail_weight.T[:, :, None]
    )
    inner_weights = (decay_mat * c_dot_b[None] * inv_root).astype(jnp.bfloat16)
    inner = jnp.einsum("hus,uhp->shp", inner_weights, grad_out, preferred_element_type=jnp.float32)
    d_x = d_x + input_scale.T[:, :, None] * inner
    return (d_x, d_b, d_c)


def state_chain(decays, adds, start, backward):

    def step(carry, item):
        return (item[0][:, None, None] * carry + item[1], carry)

    return lax.scan(step, start, (decays, adds), reverse=backward)


def local(inputs, weight_codes, scales, log_decay, cotangent):
    tok_count = inputs.shape[1]
    features = inputs[0]
    grad_out = cotangent[0]
    head_count = log_decay.shape[1]
    hp_width = grad_out.shape[1]
    head_dim = hp_width // head_count
    proj_width = weight_codes.shape[1]
    state_width = (proj_width - hp_width) // 2
    weights = lax.all_gather(dequantize(weight_codes, scales), "seq", axis=0, tiled=True)
    projected = jnp.dot(features, weights, preferred_element_type=jnp.float32).astype(jnp.bfloat16)
    block_len = min(128, tok_count)
    block_count = tok_count // block_len
    x_blocks = projected[:, :hp_width].reshape(block_count, block_len, head_count, head_dim)
    b_blocks = projected[:, hp_width : hp_width + state_width].reshape(
        block_count, block_len, state_width
    )
    c_blocks = projected[:, hp_width + state_width :].reshape(block_count, block_len, state_width)
    g_blocks = grad_out.reshape(block_count, block_len, head_count, head_dim)
    ld_blocks = log_decay[0].reshape(head_count, block_count, block_len).transpose(1, 0, 2)
    decays, fwd_states, back_states = jax.vmap(summaries)(
        x_blocks, b_blocks, c_blocks, g_blocks, ld_blocks
    )
    zero_state = jnp.zeros((head_count, state_width, head_dim), jnp.float32)
    dev_decay = jnp.prod(decays, axis=0)
    dev_fwd, unused_a = state_chain(decays, fwd_states, zero_state, False)
    dev_back, unused_b = state_chain(decays, back_states, zero_state, True)
    carried = (None, scan_entering(dev_decay, dev_fwd, "seq", False))
    returned = (None, scan_entering(dev_decay, dev_back, "seq", True))
    unused_c, state_starts = state_chain(decays, fwd_states, carried[1], False)
    unused_d, back_starts = state_chain(decays, back_states, returned[1], True)
    d_x, d_b, d_c = lax.map(
        lambda block_item: block_grads(*block_item),
        (x_blocks, b_blocks, c_blocks, g_blocks, ld_blocks, state_starts, back_starts),
    )
    d_proj = jnp.concatenate(
        [
            d_x.reshape(tok_count, hp_width),
            d_b.reshape(tok_count, state_width),
            d_c.reshape(tok_count, state_width),
        ],
        axis=1,
    ).astype(jnp.bfloat16)
    grad_in = lax.dot_general(
        d_proj, weights, (((1,), (1,)), ((), ())), preferred_element_type=jnp.float32
    )
    seq_count = lax.axis_size("seq")
    group_count = lax.axis_size("dp")
    norm_factor = 1.0 / math.sqrt(group_count * seq_count * tok_count)
    partial_grad = seq_reduce_scatter(
        lax.dot_general(
            features, d_proj, (((0,), (0,)), ((), ())), preferred_element_type=jnp.float32
        ).astype(jnp.bfloat16),
        "seq",
    )
    summed_grad = replicated_sum(partial_grad, "dp")
    return (grad_in[None], summed_grad * norm_factor)


def solution(mesh):
    placed = (
        P("dp", "seq", None),
        P("seq", None),
        P("seq", None),
        P("dp", None, "seq"),
        P("dp", "seq", None),
    )
    return jax.shard_map(
        local,
        mesh=mesh,
        in_specs=placed,
        out_specs=(P("dp", "seq", None), P("seq", None)),
        check_vma=False,
    )
```

```python
import math

import jax
import jax.numpy as jnp
from jax import lax
from jax.sharding import PartitionSpec as P


def shifted(value, axis, step, reverse):
    count = lax.axis_size(axis)
    if reverse:
        pairs = [(place, place - step) for place in range(step, count)]
    else:
        pairs = [(place, place + step) for place in range(count - step)]
    return lax.ppermute(value.astype(jnp.bfloat16), axis, pairs).astype(value.dtype)


def scan_entering(decay, state, axis, reverse):
    head_count = state.shape[0]
    flat = state.reshape(head_count, -1)
    split = flat.shape[1]
    count = lax.axis_size(axis)

    def send(part, step):
        flat, decay = part
        high = lax.reduce_precision(decay, exponent_bits=8, mantissa_bits=7)
        lanes = lambda piece: jnp.broadcast_to(piece[:, None], (head_count, 128))
        packed = jnp.concatenate([flat, lanes(high), lanes(decay - high)], axis=1)
        got = shifted(packed, axis, step, reverse)
        return got[:, :split], got[:, split] + got[:, split + 128]

    def chain(parts):
        flat, decay = parts[0]
        for later_flat, later_decay in parts[1:]:
            flat = later_decay[:, None] * flat + later_flat
            decay = decay * later_decay
        return flat, decay

    radix = 4
    own = (flat, decay)
    part = chain([send(own, step) for step in range(radix, 0, -1)])
    width = radix
    while width < count:
        pieces = min(radix, -(-count // width))
        part = chain([send(part, width * m) for m in range(pieces - 1, 0, -1)] + [part])
        width *= pieces
    flat = part[0]
    return flat.reshape(state.shape)


def butterfly_sum(value, axis):
    count = lax.axis_size(axis)
    step = 1
    while step < count:
        pairs = [(place, place ^ step) for place in range(count)]
        value = value + lax.ppermute(value, axis, pairs)
        step *= 2
    return value


def digit_reduce(value, axis, where, stride, radix):
    count = lax.axis_size(axis)
    digit = (lax.axis_index(axis) // stride) % radix
    total = lax.dynamic_index_in_dim(value, digit, where, False).astype(jnp.float32)
    for offset in range(1, radix):
        piece = lax.dynamic_index_in_dim(value, (digit + offset) % radix, where, False)
        pairs = [
            (place, place + (((place // stride) % radix + offset) % radix - (place // stride) % radix) * stride)
            for place in range(count)
        ]
        got = lax.ppermute(piece.astype(jnp.bfloat16), axis, pairs)
        total = total + got.astype(jnp.float32)
    return total


def seq_reduce_scatter(partial, axis):
    rows, cols = partial.shape
    count = lax.axis_size(axis)
    block = rows // count
    value = partial.reshape(count // 8, 4, 2, block, cols)
    value = digit_reduce(value, axis, 2, 1, 2)
    half = cols // 2
    first = digit_reduce(value[..., :half], axis, 1, 2, 4)
    first = digit_reduce(first, axis, 0, 8, count // 8)
    second = digit_reduce(value[..., half:], axis, 0, 8, count // 8)
    second = digit_reduce(second, axis, 0, 2, 4)
    return jnp.concatenate([first, second], axis=1)


def replicated_sum(value, axis):
    count = lax.axis_size(axis)
    me = lax.axis_index(axis)
    slabs = value.reshape(count, value.shape[0] // count, value.shape[1])
    total = lax.dynamic_index_in_dim(slabs, me, 0, False)
    for offset in range(1, count):
        piece = lax.dynamic_index_in_dim(slabs, (me + offset) % count, 0, False)
        pairs = [(place, (place + offset) % count) for place in range(count)]
        total = total + lax.ppermute(piece, axis, pairs)
    gathered = [total]
    for offset in range(1, count):
        pairs = [(place, (place + offset) % count) for place in range(count)]
        gathered.append(lax.ppermute(total, axis, pairs))
    stacked = jnp.stack(gathered)
    order = (me - jnp.arange(count)) % count
    return jnp.take(stacked, order, axis=0).reshape(value.shape)


def dequantize(code_rows, scale_rows):
    row_count, col_count = code_rows.shape
    group_count = scale_rows.shape[1]
    spread = code_rows.astype(jnp.float32).reshape(row_count, group_count, col_count // group_count)
    spread = spread * scale_rows.astype(jnp.float32)[:, :, None]
    return spread.reshape(row_count, col_count).astype(jnp.bfloat16)


def block_prep(ld_block):
    cum_log = jnp.cumsum(ld_block, axis=1)
    input_scale = jnp.sqrt(-jnp.expm1(2.0 * ld_block))
    tail_weight = jnp.exp(cum_log[:, -1:] - cum_log) * input_scale
    return (cum_log, input_scale, tail_weight)


def weighted_pair(x_vals, grad_out, tail_weight, cum_log, inv_root):
    head_weight = jnp.exp(cum_log) * inv_root
    weighted_x = (x_vals.astype(jnp.float32) * tail_weight.T[:, :, None]).astype(jnp.bfloat16)
    weighted_g = (grad_out.astype(jnp.float32) * head_weight.T[:, :, None]).astype(jnp.bfloat16)
    return (weighted_x, weighted_g)


def summaries(x_vals, b_mat, c_mat, grad_out, ld_block):
    cum_log, input_scale, tail_weight = block_prep(ld_block)
    inv_root = 1.0 / math.sqrt(b_mat.shape[1])
    weighted_x, weighted_g = weighted_pair(x_vals, grad_out, tail_weight, cum_log, inv_root)
    fwd_state = jnp.einsum("sn,shp->hnp", b_mat, weighted_x, preferred_element_type=jnp.float32)
    back_state = jnp.einsum("tn,thp->hnp", c_mat, weighted_g, preferred_element_type=jnp.float32)
    return (jnp.exp(cum_log[:, -1]), fwd_state, back_state)


def block_grads(x_vals, b_mat, c_mat, grad_out, ld_block, state_in, back_in):
    block_len = ld_block.shape[1]
    cum_log, input_scale, tail_weight = block_prep(ld_block)
    inv_root = 1.0 / math.sqrt(b_mat.shape[1])
    weighted_x, weighted_g = weighted_pair(x_vals, grad_out, tail_weight, cum_log, inv_root)
    row_ids = lax.broadcasted_iota(jnp.int32, (block_len, block_len), 0)
    col_ids = lax.broadcasted_iota(jnp.int32, (block_len, block_len), 1)
    lower_mask = (row_ids >= col_ids)[None]
    log_gap = cum_log[:, :, None] - cum_log[:, None, :]
    decay_mat = jnp.where(lower_mask, jnp.exp(jnp.where(lower_mask, log_gap, 0.0)), 0.0)
    state_low = state_in.astype(jnp.bfloat16)
    back_low = back_in.astype(jnp.bfloat16)
    x_dot_g = jnp.einsum("thp,shp->hts", grad_out, x_vals, preferred_element_type=jnp.float32)
    c_dot_b = jnp.dot(c_mat, b_mat.T, preferred_element_type=jnp.float32)
    mix_weights = (
        jnp.sum(decay_mat * input_scale[:, None, :] * x_dot_g, axis=0) * inv_root
    ).astype(jnp.bfloat16)
    d_c = jnp.einsum("hnp,thp->tn", state_low, weighted_g, preferred_element_type=jnp.float32)
    d_c = d_c + jnp.dot(mix_weights, b_mat, preferred_element_type=jnp.float32)
    d_b = jnp.einsum("hnp,thp->tn", back_low, weighted_x, preferred_element_type=jnp.float32)
    d_b = d_b + jnp.dot(mix_weights.T, c_mat, preferred_element_type=jnp.float32)
    d_x = (
        jnp.einsum("tn,hnp->thp", b_mat, back_low, preferred_element_type=jnp.float32)
        * tail_weight.T[:, :, None]
    )
    inner_weights = (decay_mat * c_dot_b[None] * inv_root).astype(jnp.bfloat16)
    inner = jnp.einsum("hus,uhp->shp", inner_weights, grad_out, preferred_element_type=jnp.float32)
    d_x = d_x + input_scale.T[:, :, None] * inner
    return (d_x, d_b, d_c)


def state_chain(decays, adds, start, backward):

    def step(carry, item):
        return (item[0][:, None, None] * carry + item[1], carry)

    return lax.scan(step, start, (decays, adds), reverse=backward)


def local(inputs, weight_codes, scales, log_decay, cotangent):
    tok_count = inputs.shape[1]
    features = inputs[0]
    grad_out = cotangent[0]
    head_count = log_decay.shape[1]
    hp_width = grad_out.shape[1]
    head_dim = hp_width // head_count
    proj_width = weight_codes.shape[1]
    state_width = (proj_width - hp_width) // 2
    weights = lax.all_gather(dequantize(weight_codes, scales), "seq", axis=0, tiled=True)
    projected = jnp.dot(features, weights, preferred_element_type=jnp.float32).astype(jnp.bfloat16)
    block_len = min(128, tok_count)
    block_count = tok_count // block_len
    x_blocks = projected[:, :hp_width].reshape(block_count, block_len, head_count, head_dim)
    b_blocks = projected[:, hp_width : hp_width + state_width].reshape(
        block_count, block_len, state_width
    )
    c_blocks = projected[:, hp_width + state_width :].reshape(block_count, block_len, state_width)
    g_blocks = grad_out.reshape(block_count, block_len, head_count, head_dim)
    ld_blocks = log_decay[0].reshape(head_count, block_count, block_len).transpose(1, 0, 2)
    decays, fwd_states, back_states = jax.vmap(summaries)(
        x_blocks, b_blocks, c_blocks, g_blocks, ld_blocks
    )
    zero_state = jnp.zeros((head_count, state_width, head_dim), jnp.float32)
    dev_decay = jnp.prod(decays, axis=0)
    dev_fwd, unused_a = state_chain(decays, fwd_states, zero_state, False)
    dev_back, unused_b = state_chain(decays, back_states, zero_state, True)
    carried = (None, scan_entering(dev_decay, dev_fwd, "seq", False))
    returned = (None, scan_entering(dev_decay, dev_back, "seq", True))
    unused_c, state_starts = state_chain(decays, fwd_states, carried[1], False)
    unused_d, back_starts = state_chain(decays, back_states, returned[1], True)
    d_x, d_b, d_c = lax.map(
        lambda block_item: block_grads(*block_item),
        (x_blocks, b_blocks, c_blocks, g_blocks, ld_blocks, state_starts, back_starts),
    )
    d_proj = jnp.concatenate(
        [
            d_x.reshape(tok_count, hp_width),
            d_b.reshape(tok_count, state_width),
            d_c.reshape(tok_count, state_width),
        ],
        axis=1,
    ).astype(jnp.bfloat16)
    grad_in = lax.dot_general(
        d_proj, weights, (((1,), (1,)), ((), ())), preferred_element_type=jnp.float32
    )
    seq_count = lax.axis_size("seq")
    group_count = lax.axis_size("dp")
    norm_factor = 1.0 / math.sqrt(group_count * seq_count * tok_count)
    partial_grad = seq_reduce_scatter(
        lax.dot_general(
            features, d_proj, (((0,), (0,)), ((), ())), preferred_element_type=jnp.float32
        ).astype(jnp.bfloat16),
        "seq",
    )
    summed_grad = replicated_sum(partial_grad, "dp")
    return (grad_in[None], summed_grad * norm_factor)


def solution(mesh):
    placed = (
        P("dp", "seq", None),
        P("seq", None),
        P("seq", None),
        P("dp", None, "seq"),
        P("dp", "seq", None),
    )
    return jax.shard_map(
        local,
        mesh=mesh,
        in_specs=placed,
        out_specs=(P("dp", "seq", None), P("seq", None)),
        check_vma=False,
    )
```

```python
import math

import jax
import jax.numpy as jnp
from jax import lax
from jax.sharding import PartitionSpec as P


def shifted(value, axis, step, reverse):
    count = lax.axis_size(axis)
    if reverse:
        pairs = [(place, place - step) for place in range(step, count)]
    else:
        pairs = [(place, place + step) for place in range(count - step)]
    return lax.ppermute(value.astype(jnp.bfloat16), axis, pairs).astype(value.dtype)


def scan_entering(decay, state, axis, reverse, hold=None):
    head_count = state.shape[0]
    flat = state.reshape(head_count, -1)
    split = flat.shape[1]
    count = lax.axis_size(axis)

    def send(part, step):
        flat, decay = part
        high = lax.reduce_precision(decay, exponent_bits=8, mantissa_bits=7)
        lanes = lambda piece: jnp.broadcast_to(piece[:, None], (head_count, 128))
        packed = jnp.concatenate([flat, lanes(high), lanes(decay - high)], axis=1)
        got = shifted(packed, axis, step, reverse)
        return got[:, :split], got[:, split] + got[:, split + 128]

    def chain(parts):
        flat, decay = parts[0]
        for later_flat, later_decay in parts[1:]:
            flat = later_decay[:, None] * flat + later_flat
            decay = decay * later_decay
        return flat, decay

    radix = 4
    held = hold
    own = (flat, decay)
    part = chain([send(own, step) for step in range(radix, 0, -1)])
    width = radix
    while width < count:
        pieces = min(radix, -(-count // width))
        part = chain([send(part, width * m) for m in range(pieces - 1, 0, -1)] + [part])
        width *= pieces
        if hold is not None:
            part, held = lax.optimization_barrier((part, hold))
            hold = None
    flat = part[0]
    return flat.reshape(state.shape), held


def butterfly_sum(value, axis):
    count = lax.axis_size(axis)
    step = 1
    while step < count:
        pairs = [(place, place ^ step) for place in range(count)]
        value = value + lax.ppermute(value, axis, pairs)
        step *= 2
    return value


def digit_reduce(value, axis, where, stride, radix):
    count = lax.axis_size(axis)
    digit = (lax.axis_index(axis) // stride) % radix
    total = lax.dynamic_index_in_dim(value, digit, where, False).astype(jnp.float32)
    for offset in range(1, radix):
        piece = lax.dynamic_index_in_dim(value, (digit + offset) % radix, where, False)
        pairs = [
            (place, place + (((place // stride) % radix + offset) % radix - (place // stride) % radix) * stride)
            for place in range(count)
        ]
        got = lax.ppermute(piece.astype(jnp.bfloat16), axis, pairs)
        total = total + got.astype(jnp.float32)
    return total


def seq_reduce_scatter(partial, axis):
    rows, cols = partial.shape
    count = lax.axis_size(axis)
    block = rows // count
    value = partial.reshape(count // 8, 4, 2, block, cols)
    value = digit_reduce(value, axis, 2, 1, 2)
    half = cols // 2
    first = digit_reduce(value[..., :half], axis, 1, 2, 4)
    first = digit_reduce(first, axis, 0, 8, count // 8)
    second = digit_reduce(value[..., half:], axis, 0, 8, count // 8)
    second = digit_reduce(second, axis, 0, 2, 4)
    return jnp.concatenate([first, second], axis=1)


def replicated_sum(value, axis):
    count = lax.axis_size(axis)
    me = lax.axis_index(axis)
    slabs = value.reshape(count, value.shape[0] // count, value.shape[1])
    total = lax.dynamic_index_in_dim(slabs, me, 0, False)
    for offset in range(1, count):
        piece = lax.dynamic_index_in_dim(slabs, (me + offset) % count, 0, False)
        pairs = [(place, (place + offset) % count) for place in range(count)]
        total = total + lax.ppermute(piece, axis, pairs)
    gathered = [total]
    for offset in range(1, count):
        pairs = [(place, (place + offset) % count) for place in range(count)]
        gathered.append(lax.ppermute(total, axis, pairs))
    stacked = jnp.stack(gathered)
    order = (me - jnp.arange(count)) % count
    return jnp.take(stacked, order, axis=0).reshape(value.shape)


def dequantize(code_rows, scale_rows):
    row_count, col_count = code_rows.shape
    group_count = scale_rows.shape[1]
    spread = code_rows.astype(jnp.float32).reshape(row_count, group_count, col_count // group_count)
    spread = spread * scale_rows.astype(jnp.float32)[:, :, None]
    return spread.reshape(row_count, col_count).astype(jnp.bfloat16)


def block_prep(ld_block):
    cum_log = jnp.cumsum(ld_block, axis=1)
    input_scale = jnp.sqrt(-jnp.expm1(2.0 * ld_block))
    tail_weight = jnp.exp(cum_log[:, -1:] - cum_log) * input_scale
    return (cum_log, input_scale, tail_weight)


def weighted_pair(x_vals, grad_out, tail_weight, cum_log, inv_root):
    head_weight = jnp.exp(cum_log) * inv_root
    weighted_x = (x_vals.astype(jnp.float32) * tail_weight.T[:, :, None]).astype(jnp.bfloat16)
    weighted_g = (grad_out.astype(jnp.float32) * head_weight.T[:, :, None]).astype(jnp.bfloat16)
    return (weighted_x, weighted_g)


def summaries(x_vals, b_mat, c_mat, grad_out, ld_block):
    cum_log, input_scale, tail_weight = block_prep(ld_block)
    inv_root = 1.0 / math.sqrt(b_mat.shape[1])
    weighted_x, weighted_g = weighted_pair(x_vals, grad_out, tail_weight, cum_log, inv_root)
    fwd_state = jnp.einsum("sn,shp->hnp", b_mat, weighted_x, preferred_element_type=jnp.float32)
    back_state = jnp.einsum("tn,thp->hnp", c_mat, weighted_g, preferred_element_type=jnp.float32)
    return (jnp.exp(cum_log[:, -1]), fwd_state, back_state)


def back_summary(c_mat, grad_out, ld_block):
    cum_log, input_scale, tail_weight = block_prep(ld_block)
    inv_root = 1.0 / math.sqrt(c_mat.shape[1])
    head_weight = jnp.exp(cum_log) * inv_root
    weighted_g = (grad_out.astype(jnp.float32) * head_weight.T[:, :, None]).astype(jnp.bfloat16)
    return jnp.einsum("tn,thp->hnp", c_mat, weighted_g, preferred_element_type=jnp.float32)


def block_grads(x_vals, b_mat, c_mat, grad_out, ld_block, state_in, back_in):
    block_len = ld_block.shape[1]
    cum_log, input_scale, tail_weight = block_prep(ld_block)
    inv_root = 1.0 / math.sqrt(b_mat.shape[1])
    weighted_x, weighted_g = weighted_pair(x_vals, grad_out, tail_weight, cum_log, inv_root)
    row_ids = lax.broadcasted_iota(jnp.int32, (block_len, block_len), 0)
    col_ids = lax.broadcasted_iota(jnp.int32, (block_len, block_len), 1)
    lower_mask = (row_ids >= col_ids)[None]
    log_gap = cum_log[:, :, None] - cum_log[:, None, :]
    decay_mat = jnp.where(lower_mask, jnp.exp(jnp.where(lower_mask, log_gap, 0.0)), 0.0)
    state_low = state_in.astype(jnp.bfloat16)
    back_low = back_in.astype(jnp.bfloat16)
    x_dot_g = jnp.einsum("thp,shp->hts", grad_out, x_vals, preferred_element_type=jnp.float32)
    c_dot_b = jnp.dot(c_mat, b_mat.T, preferred_element_type=jnp.float32)
    mix_weights = (
        jnp.sum(decay_mat * input_scale[:, None, :] * x_dot_g, axis=0) * inv_root
    ).astype(jnp.bfloat16)
    d_c = jnp.einsum("hnp,thp->tn", state_low, weighted_g, preferred_element_type=jnp.float32)
    d_c = d_c + jnp.dot(mix_weights, b_mat, preferred_element_type=jnp.float32)
    d_b = jnp.einsum("hnp,thp->tn", back_low, weighted_x, preferred_element_type=jnp.float32)
    d_b = d_b + jnp.dot(mix_weights.T, c_mat, preferred_element_type=jnp.float32)
    d_x = (
        jnp.einsum("tn,hnp->thp", b_mat, back_low, preferred_element_type=jnp.float32)
        * tail_weight.T[:, :, None]
    )
    inner_weights = (decay_mat * c_dot_b[None] * inv_root).astype(jnp.bfloat16)
    inner = jnp.einsum("hus,uhp->shp", inner_weights, grad_out, preferred_element_type=jnp.float32)
    d_x = d_x + input_scale.T[:, :, None] * inner
    return (d_x, d_b, d_c)


def state_chain(decays, adds, start, backward):

    def step(carry, item):
        return (item[0][:, None, None] * carry + item[1], carry)

    return lax.scan(step, start, (decays, adds), reverse=backward)


def local(inputs, weight_codes, scales, log_decay, cotangent):
    tok_count = inputs.shape[1]
    features = inputs[0]
    grad_out = cotangent[0]
    head_count = log_decay.shape[1]
    hp_width = grad_out.shape[1]
    head_dim = hp_width // head_count
    proj_width = weight_codes.shape[1]
    state_width = (proj_width - hp_width) // 2
    local_weights = dequantize(weight_codes, scales)
    state_weights = lax.all_gather(local_weights[:, hp_width:], "seq", axis=0, tiled=True)
    head_weights = lax.all_gather(local_weights[:, :hp_width], "seq", axis=0, tiled=True)
    state_proj = jnp.dot(features, state_weights, preferred_element_type=jnp.float32).astype(
        jnp.bfloat16
    )
    block_len = min(128, tok_count)
    block_count = tok_count // block_len
    b_blocks = state_proj[:, :state_width].reshape(block_count, block_len, state_width)
    c_blocks = state_proj[:, state_width:].reshape(block_count, block_len, state_width)
    g_blocks = grad_out.reshape(block_count, block_len, head_count, head_dim)
    ld_blocks = log_decay[0].reshape(head_count, block_count, block_len).transpose(1, 0, 2)
    zero_state = jnp.zeros((head_count, state_width, head_dim), jnp.float32)
    back_states = jax.vmap(back_summary)(c_blocks, g_blocks, ld_blocks)
    decays = jnp.exp(jnp.cumsum(ld_blocks, axis=2)[:, :, -1])
    dev_decay = jnp.prod(decays, axis=0)
    dev_back, unused_b = state_chain(decays, back_states, zero_state, True)
    back_entering, head_weights = scan_entering(dev_decay, dev_back, "seq", True, head_weights)
    returned = (None, back_entering)
    weights = jnp.concatenate([head_weights, state_weights], axis=1)
    head_proj = jnp.dot(features, head_weights, preferred_element_type=jnp.float32).astype(
        jnp.bfloat16
    )
    x_blocks = head_proj.reshape(block_count, block_len, head_count, head_dim)
    unused_e, fwd_states, unused_f = jax.vmap(summaries)(
        x_blocks, b_blocks, c_blocks, g_blocks, ld_blocks
    )
    dev_fwd, unused_a = state_chain(decays, fwd_states, zero_state, False)
    carried = (None, scan_entering(dev_decay, dev_fwd, "seq", False)[0])
    unused_c, state_starts = state_chain(decays, fwd_states, carried[1], False)
    unused_d, back_starts = state_chain(decays, back_states, returned[1], True)
    d_x, d_b, d_c = lax.map(
        lambda block_item: block_grads(*block_item),
        (x_blocks, b_blocks, c_blocks, g_blocks, ld_blocks, state_starts, back_starts),
    )
    d_proj = jnp.concatenate(
        [
            d_x.reshape(tok_count, hp_width),
            d_b.reshape(tok_count, state_width),
            d_c.reshape(tok_count, state_width),
        ],
        axis=1,
    ).astype(jnp.bfloat16)
    grad_in = lax.dot_general(
        d_proj, weights, (((1,), (1,)), ((), ())), preferred_element_type=jnp.float32
    )
    seq_count = lax.axis_size("seq")
    group_count = lax.axis_size("dp")
    norm_factor = 1.0 / math.sqrt(group_count * seq_count * tok_count)
    partial_grad = seq_reduce_scatter(
        lax.dot_general(
            features, d_proj, (((0,), (0,)), ((), ())), preferred_element_type=jnp.float32
        ).astype(jnp.bfloat16),
        "seq",
    )
    summed_grad = replicated_sum(partial_grad, "dp")
    return (grad_in[None], summed_grad * norm_factor)


def solution(mesh):
    placed = (
        P("dp", "seq", None),
        P("seq", None),
        P("seq", None),
        P("dp", None, "seq"),
        P("dp", "seq", None),
    )
    return jax.shard_map(
        local,
        mesh=mesh,
        in_specs=placed,
        out_specs=(P("dp", "seq", None), P("seq", None)),
        check_vma=False,
    )
```

```python
import math

import jax
import jax.numpy as jnp
from jax import lax
from jax.sharding import PartitionSpec as P


def shifted(value, axis, step, reverse):
    count = lax.axis_size(axis)
    if reverse:
        pairs = [(place, place - step) for place in range(step, count)]
    else:
        pairs = [(place, place + step) for place in range(count - step)]
    return lax.ppermute(value.astype(jnp.bfloat16), axis, pairs).astype(value.dtype)


def scan_entering(decay, state, axis, reverse):
    head_count = state.shape[0]
    flat = state.reshape(head_count, -1)
    split = flat.shape[1]
    count = lax.axis_size(axis)

    def send(part, step):
        flat, decay = part
        high = lax.reduce_precision(decay, exponent_bits=8, mantissa_bits=7)
        lanes = lambda piece: jnp.broadcast_to(piece[:, None], (head_count, 128))
        packed = jnp.concatenate([flat, lanes(high), lanes(decay - high)], axis=1)
        got = shifted(packed, axis, step, reverse)
        return got[:, :split], got[:, split] + got[:, split + 128]

    def chain(parts):
        flat, decay = parts[0]
        for later_flat, later_decay in parts[1:]:
            flat = later_decay[:, None] * flat + later_flat
            decay = decay * later_decay
        return flat, decay

    radix = 4
    own = (flat, decay)
    part = chain([send(own, step) for step in range(radix, 0, -1)])
    width = radix
    while width < count:
        pieces = min(radix, -(-count // width))
        part = chain([send(part, width * m) for m in range(pieces - 1, 0, -1)] + [part])
        width *= pieces
    flat = part[0]
    return flat.reshape(state.shape)


def butterfly_sum(value, axis):
    count = lax.axis_size(axis)
    step = 1
    while step < count:
        pairs = [(place, place ^ step) for place in range(count)]
        value = value + lax.ppermute(value, axis, pairs)
        step *= 2
    return value


def digit_reduce(value, axis, where, stride, radix):
    count = lax.axis_size(axis)
    digit = (lax.axis_index(axis) // stride) % radix
    total = lax.dynamic_index_in_dim(value, digit, where, False).astype(jnp.float32)
    for offset in range(1, radix):
        piece = lax.dynamic_index_in_dim(value, (digit + offset) % radix, where, False)
        pairs = [
            (place, place + (((place // stride) % radix + offset) % radix - (place // stride) % radix) * stride)
            for place in range(count)
        ]
        got = lax.ppermute(piece.astype(jnp.bfloat16), axis, pairs)
        total = total + got.astype(jnp.float32)
    return total


def seq_reduce_scatter(partial, axis):
    rows, cols = partial.shape
    count = lax.axis_size(axis)
    block = rows // count
    value = partial.reshape(count // 8, 4, 2, block, cols)
    value = digit_reduce(value, axis, 2, 1, 2)
    half = cols // 2
    first = digit_reduce(value[..., :half], axis, 1, 2, 4)
    first = digit_reduce(first, axis, 0, 8, count // 8)
    second = digit_reduce(value[..., half:], axis, 0, 8, count // 8)
    second = digit_reduce(second, axis, 0, 2, 4)
    return jnp.concatenate([first, second], axis=1)


def replicated_sum(value, axis):
    count = lax.axis_size(axis)
    me = lax.axis_index(axis)
    slabs = value.reshape(count, value.shape[0] // count, value.shape[1])
    total = lax.dynamic_index_in_dim(slabs, me, 0, False)
    for offset in range(1, count):
        piece = lax.dynamic_index_in_dim(slabs, (me + offset) % count, 0, False)
        pairs = [(place, (place + offset) % count) for place in range(count)]
        total = total + lax.ppermute(piece, axis, pairs)
    gathered = [total]
    for offset in range(1, count):
        pairs = [(place, (place + offset) % count) for place in range(count)]
        gathered.append(lax.ppermute(total, axis, pairs))
    stacked = jnp.stack(gathered)
    order = (me - jnp.arange(count)) % count
    return jnp.take(stacked, order, axis=0).reshape(value.shape)


def dequantize(code_rows, scale_rows):
    row_count, col_count = code_rows.shape
    group_count = scale_rows.shape[1]
    spread = code_rows.astype(jnp.float32).reshape(row_count, group_count, col_count // group_count)
    spread = spread * scale_rows.astype(jnp.float32)[:, :, None]
    return spread.reshape(row_count, col_count).astype(jnp.bfloat16)


def block_prep(ld_block):
    cum_log = jnp.cumsum(ld_block, axis=1)
    input_scale = jnp.sqrt(-jnp.expm1(2.0 * ld_block))
    tail_weight = jnp.exp(cum_log[:, -1:] - cum_log) * input_scale
    return (cum_log, input_scale, tail_weight)


def weighted_pair(x_vals, grad_out, tail_weight, cum_log, inv_root):
    head_weight = jnp.exp(cum_log) * inv_root
    weighted_x = (x_vals.astype(jnp.float32) * tail_weight.T[:, :, None]).astype(jnp.bfloat16)
    weighted_g = (grad_out.astype(jnp.float32) * head_weight.T[:, :, None]).astype(jnp.bfloat16)
    return (weighted_x, weighted_g)


def summaries(x_vals, b_mat, c_mat, grad_out, ld_block):
    cum_log, input_scale, tail_weight = block_prep(ld_block)
    inv_root = 1.0 / math.sqrt(b_mat.shape[1])
    weighted_x, weighted_g = weighted_pair(x_vals, grad_out, tail_weight, cum_log, inv_root)
    fwd_state = jnp.einsum("sn,shp->hnp", b_mat, weighted_x, preferred_element_type=jnp.float32)
    back_state = jnp.einsum("tn,thp->hnp", c_mat, weighted_g, preferred_element_type=jnp.float32)
    return (jnp.exp(cum_log[:, -1]), fwd_state, back_state)


def block_grads(x_vals, b_mat, c_mat, grad_out, ld_block, state_in, back_in):
    block_len = ld_block.shape[1]
    cum_log, input_scale, tail_weight = block_prep(ld_block)
    inv_root = 1.0 / math.sqrt(b_mat.shape[1])
    weighted_x, weighted_g = weighted_pair(x_vals, grad_out, tail_weight, cum_log, inv_root)
    row_ids = lax.broadcasted_iota(jnp.int32, (block_len, block_len), 0)
    col_ids = lax.broadcasted_iota(jnp.int32, (block_len, block_len), 1)
    lower_mask = (row_ids >= col_ids)[None]
    log_gap = cum_log[:, :, None] - cum_log[:, None, :]
    decay_mat = jnp.where(lower_mask, jnp.exp(jnp.where(lower_mask, log_gap, 0.0)), 0.0)
    state_low = state_in.astype(jnp.bfloat16)
    back_low = back_in.astype(jnp.bfloat16)
    x_dot_g = jnp.einsum("thp,shp->hts", grad_out, x_vals, preferred_element_type=jnp.float32)
    c_dot_b = jnp.dot(c_mat, b_mat.T, preferred_element_type=jnp.float32)
    mix_weights = (
        jnp.sum(decay_mat * input_scale[:, None, :] * x_dot_g, axis=0) * inv_root
    ).astype(jnp.bfloat16)
    d_c = jnp.einsum("hnp,thp->tn", state_low, weighted_g, preferred_element_type=jnp.float32)
    d_c = d_c + jnp.dot(mix_weights, b_mat, preferred_element_type=jnp.float32)
    d_b = jnp.einsum("hnp,thp->tn", back_low, weighted_x, preferred_element_type=jnp.float32)
    d_b = d_b + jnp.dot(mix_weights.T, c_mat, preferred_element_type=jnp.float32)
    d_x = (
        jnp.einsum("tn,hnp->thp", b_mat, back_low, preferred_element_type=jnp.float32)
        * tail_weight.T[:, :, None]
    )
    inner_weights = (decay_mat * c_dot_b[None] * inv_root).astype(jnp.bfloat16)
    inner = jnp.einsum("hus,uhp->shp", inner_weights, grad_out, preferred_element_type=jnp.float32)
    d_x = d_x + input_scale.T[:, :, None] * inner
    return (d_x, d_b, d_c)


def state_chain(decays, adds, start, backward):

    def step(carry, item):
        return (item[0][:, None, None] * carry + item[1], carry)

    return lax.scan(step, start, (decays, adds), reverse=backward)


def local(inputs, weight_codes, scales, log_decay, cotangent):
    tok_count = inputs.shape[1]
    features = inputs[0]
    grad_out = cotangent[0]
    head_count = log_decay.shape[1]
    hp_width = grad_out.shape[1]
    head_dim = hp_width // head_count
    proj_width = weight_codes.shape[1]
    state_width = (proj_width - hp_width) // 2
    local_weights = dequantize(weight_codes, scales)
    seq_count = lax.axis_size("seq")
    spread = jnp.broadcast_to(local_weights[None], (seq_count,) + local_weights.shape)
    weights = lax.all_to_all(spread, "seq", 0, 0, tiled=False).reshape(-1, proj_width)
    projected = jnp.dot(features, weights, preferred_element_type=jnp.float32).astype(jnp.bfloat16)
    block_len = min(128, tok_count)
    block_count = tok_count // block_len
    x_blocks = projected[:, :hp_width].reshape(block_count, block_len, head_count, head_dim)
    b_blocks = projected[:, hp_width : hp_width + state_width].reshape(
        block_count, block_len, state_width
    )
    c_blocks = projected[:, hp_width + state_width :].reshape(block_count, block_len, state_width)
    g_blocks = grad_out.reshape(block_count, block_len, head_count, head_dim)
    ld_blocks = log_decay[0].reshape(head_count, block_count, block_len).transpose(1, 0, 2)
    decays, fwd_states, back_states = jax.vmap(summaries)(
        x_blocks, b_blocks, c_blocks, g_blocks, ld_blocks
    )
    zero_state = jnp.zeros((head_count, state_width, head_dim), jnp.float32)
    dev_decay = jnp.prod(decays, axis=0)
    dev_fwd, unused_a = state_chain(decays, fwd_states, zero_state, False)
    dev_back, unused_b = state_chain(decays, back_states, zero_state, True)
    carried = (None, scan_entering(dev_decay, dev_fwd, "seq", False))
    returned = (None, scan_entering(dev_decay, dev_back, "seq", True))
    unused_c, state_starts = state_chain(decays, fwd_states, carried[1], False)
    unused_d, back_starts = state_chain(decays, back_states, returned[1], True)
    d_x, d_b, d_c = lax.map(
        lambda block_item: block_grads(*block_item),
        (x_blocks, b_blocks, c_blocks, g_blocks, ld_blocks, state_starts, back_starts),
    )
    d_proj = jnp.concatenate(
        [
            d_x.reshape(tok_count, hp_width),
            d_b.reshape(tok_count, state_width),
            d_c.reshape(tok_count, state_width),
        ],
        axis=1,
    ).astype(jnp.bfloat16)
    grad_in = lax.dot_general(
        d_proj, weights, (((1,), (1,)), ((), ())), preferred_element_type=jnp.float32
    )
    seq_count = lax.axis_size("seq")
    group_count = lax.axis_size("dp")
    norm_factor = 1.0 / math.sqrt(group_count * seq_count * tok_count)
    partial_grad = seq_reduce_scatter(
        lax.dot_general(
            features, d_proj, (((0,), (0,)), ((), ())), preferred_element_type=jnp.float32
        ).astype(jnp.bfloat16),
        "seq",
    )
    summed_grad = replicated_sum(partial_grad, "dp")
    return (grad_in[None], summed_grad * norm_factor)


def solution(mesh):
    placed = (
        P("dp", "seq", None),
        P("seq", None),
        P("seq", None),
        P("dp", None, "seq"),
        P("dp", "seq", None),
    )
    return jax.shard_map(
        local,
        mesh=mesh,
        in_specs=placed,
        out_specs=(P("dp", "seq", None), P("seq", None)),
        check_vma=False,
    )
```

```python
import math

import jax
import jax.numpy as jnp
from jax import lax
from jax.sharding import PartitionSpec as P
from jax.experimental import pallas as pl
from jax.experimental.pallas import tpu as pltpu


def shifted(value, axis, step, reverse):
    count = lax.axis_size(axis)
    if reverse:
        pairs = [(place, place - step) for place in range(step, count)]
    else:
        pairs = [(place, place + step) for place in range(count - step)]
    return lax.ppermute(value.astype(jnp.bfloat16), axis, pairs).astype(value.dtype)


def scan_entering(decay, state, axis, reverse):
    head_count = state.shape[0]
    flat = state.reshape(head_count, -1)
    split = flat.shape[1]
    count = lax.axis_size(axis)

    def send(part, step):
        flat, decay = part
        high = lax.reduce_precision(decay, exponent_bits=8, mantissa_bits=7)
        lanes = lambda piece: jnp.broadcast_to(piece[:, None], (head_count, 128))
        packed = jnp.concatenate([flat, lanes(high), lanes(decay - high)], axis=1)
        got = shifted(packed, axis, step, reverse)
        return got[:, :split], got[:, split] + got[:, split + 128]

    def chain(parts):
        flat, decay = parts[0]
        for later_flat, later_decay in parts[1:]:
            flat = later_decay[:, None] * flat + later_flat
            decay = decay * later_decay
        return flat, decay

    radix = 4
    own = (flat, decay)
    part = chain([send(own, step) for step in range(radix, 0, -1)])
    width = radix
    while width < count:
        pieces = min(radix, -(-count // width))
        part = chain([send(part, width * m) for m in range(pieces - 1, 0, -1)] + [part])
        width *= pieces
    flat = part[0]
    return flat.reshape(state.shape)


def butterfly_sum(value, axis):
    count = lax.axis_size(axis)
    step = 1
    while step < count:
        pairs = [(place, place ^ step) for place in range(count)]
        value = value + lax.ppermute(value, axis, pairs)
        step *= 2
    return value


def digit_reduce(value, axis, where, stride, radix):
    count = lax.axis_size(axis)
    digit = (lax.axis_index(axis) // stride) % radix
    total = lax.dynamic_index_in_dim(value, digit, where, False).astype(jnp.float32)
    for offset in range(1, radix):
        piece = lax.dynamic_index_in_dim(value, (digit + offset) % radix, where, False)
        pairs = [
            (place, place + (((place // stride) % radix + offset) % radix - (place // stride) % radix) * stride)
            for place in range(count)
        ]
        got = lax.ppermute(piece.astype(jnp.bfloat16), axis, pairs)
        total = total + got.astype(jnp.float32)
    return total


def seq_reduce_scatter(partial, axis):
    rows, cols = partial.shape
    count = lax.axis_size(axis)
    block = rows // count
    value = partial.reshape(count // 8, 4, 2, block, cols)
    value = digit_reduce(value, axis, 2, 1, 2)
    half = cols // 2
    first = digit_reduce(value[..., :half], axis, 1, 2, 4)
    first = digit_reduce(first, axis, 0, 8, count // 8)
    second = digit_reduce(value[..., half:], axis, 0, 8, count // 8)
    second = digit_reduce(second, axis, 0, 2, 4)
    return jnp.concatenate([first, second], axis=1)


def replicated_sum(value, axis):
    count = lax.axis_size(axis)
    me = lax.axis_index(axis)
    slabs = value.reshape(count, value.shape[0] // count, value.shape[1])
    total = lax.dynamic_index_in_dim(slabs, me, 0, False)
    for offset in range(1, count):
        piece = lax.dynamic_index_in_dim(slabs, (me + offset) % count, 0, False)
        pairs = [(place, (place + offset) % count) for place in range(count)]
        total = total + lax.ppermute(piece, axis, pairs)
    gathered = [total]
    for offset in range(1, count):
        pairs = [(place, (place + offset) % count) for place in range(count)]
        gathered.append(lax.ppermute(total, axis, pairs))
    stacked = jnp.stack(gathered)
    order = (me - jnp.arange(count)) % count
    return jnp.take(stacked, order, axis=0).reshape(value.shape)


def outer_kernel(left_ref, right_ref, out_ref):
    out_ref[...] = lax.dot_general(
        left_ref[...], right_ref[...], (((0,), (0,)), ((), ())), preferred_element_type=jnp.float32
    ).astype(out_ref.dtype)


def outer_product(left, right):
    depth, rows = left.shape
    cols = right.shape[1]
    tile = 256
    return pl.pallas_call(
        outer_kernel,
        grid=(rows // tile,),
        in_specs=[
            pl.BlockSpec((depth, tile), lambda i: (0, i)),
            pl.BlockSpec((depth, cols), lambda i: (0, 0)),
        ],
        out_specs=pl.BlockSpec((tile, cols), lambda i: (i, 0)),
        out_shape=jax.ShapeDtypeStruct((rows, cols), jnp.bfloat16),
        cost_estimate=pl.CostEstimate(
            flops=2 * depth * rows * cols,
            bytes_accessed=2 * (depth * rows + depth * cols + rows * cols),
            transcendentals=0,
        ),
    )(left, right)


def dequantize(code_rows, scale_rows):
    row_count, col_count = code_rows.shape
    group_count = scale_rows.shape[1]
    spread = code_rows.astype(jnp.float32).reshape(row_count, group_count, col_count // group_count)
    spread = spread * scale_rows.astype(jnp.float32)[:, :, None]
    return spread.reshape(row_count, col_count).astype(jnp.bfloat16)


def block_prep(ld_block):
    cum_log = jnp.cumsum(ld_block, axis=1)
    input_scale = jnp.sqrt(-jnp.expm1(2.0 * ld_block))
    tail_weight = jnp.exp(cum_log[:, -1:] - cum_log) * input_scale
    return (cum_log, input_scale, tail_weight)


def weighted_pair(x_vals, grad_out, tail_weight, cum_log, inv_root):
    head_weight = jnp.exp(cum_log) * inv_root
    weighted_x = (x_vals.astype(jnp.float32) * tail_weight.T[:, :, None]).astype(jnp.bfloat16)
    weighted_g = (grad_out.astype(jnp.float32) * head_weight.T[:, :, None]).astype(jnp.bfloat16)
    return (weighted_x, weighted_g)


def summaries(x_vals, b_mat, c_mat, grad_out, ld_block):
    cum_log, input_scale, tail_weight = block_prep(ld_block)
    inv_root = 1.0 / math.sqrt(b_mat.shape[1])
    weighted_x, weighted_g = weighted_pair(x_vals, grad_out, tail_weight, cum_log, inv_root)
    fwd_state = jnp.einsum("sn,shp->hnp", b_mat, weighted_x, preferred_element_type=jnp.float32)
    back_state = jnp.einsum("tn,thp->hnp", c_mat, weighted_g, preferred_element_type=jnp.float32)
    return (jnp.exp(cum_log[:, -1]), fwd_state, back_state)


def block_grads(x_vals, b_mat, c_mat, grad_out, ld_block, state_in, back_in):
    block_len = ld_block.shape[1]
    cum_log, input_scale, tail_weight = block_prep(ld_block)
    inv_root = 1.0 / math.sqrt(b_mat.shape[1])
    weighted_x, weighted_g = weighted_pair(x_vals, grad_out, tail_weight, cum_log, inv_root)
    row_ids = lax.broadcasted_iota(jnp.int32, (block_len, block_len), 0)
    col_ids = lax.broadcasted_iota(jnp.int32, (block_len, block_len), 1)
    lower_mask = (row_ids >= col_ids)[None]
    log_gap = cum_log[:, :, None] - cum_log[:, None, :]
    decay_mat = jnp.where(lower_mask, jnp.exp(jnp.where(lower_mask, log_gap, 0.0)), 0.0)
    state_low = state_in.astype(jnp.bfloat16)
    back_low = back_in.astype(jnp.bfloat16)
    x_dot_g = jnp.einsum("thp,shp->hts", grad_out, x_vals, preferred_element_type=jnp.float32)
    c_dot_b = jnp.dot(c_mat, b_mat.T, preferred_element_type=jnp.float32)
    mix_weights = (
        jnp.sum(decay_mat * input_scale[:, None, :] * x_dot_g, axis=0) * inv_root
    ).astype(jnp.bfloat16)
    d_c = jnp.einsum("hnp,thp->tn", state_low, weighted_g, preferred_element_type=jnp.float32)
    d_c = d_c + jnp.dot(mix_weights, b_mat, preferred_element_type=jnp.float32)
    d_b = jnp.einsum("hnp,thp->tn", back_low, weighted_x, preferred_element_type=jnp.float32)
    d_b = d_b + jnp.dot(mix_weights.T, c_mat, preferred_element_type=jnp.float32)
    d_x = (
        jnp.einsum("tn,hnp->thp", b_mat, back_low, preferred_element_type=jnp.float32)
        * tail_weight.T[:, :, None]
    )
    inner_weights = (decay_mat * c_dot_b[None] * inv_root).astype(jnp.bfloat16)
    inner = jnp.einsum("hus,uhp->shp", inner_weights, grad_out, preferred_element_type=jnp.float32)
    d_x = d_x + input_scale.T[:, :, None] * inner
    return (d_x, d_b, d_c)


def state_chain(decays, adds, start, backward):

    def step(carry, item):
        return (item[0][:, None, None] * carry + item[1], carry)

    return lax.scan(step, start, (decays, adds), reverse=backward)


def local(inputs, weight_codes, scales, log_decay, cotangent):
    tok_count = inputs.shape[1]
    features = inputs[0]
    grad_out = cotangent[0]
    head_count = log_decay.shape[1]
    hp_width = grad_out.shape[1]
    head_dim = hp_width // head_count
    proj_width = weight_codes.shape[1]
    state_width = (proj_width - hp_width) // 2
    weights = lax.all_gather(dequantize(weight_codes, scales), "seq", axis=0, tiled=True)
    projected = jnp.dot(features, weights, preferred_element_type=jnp.float32).astype(jnp.bfloat16)
    block_len = min(128, tok_count)
    block_count = tok_count // block_len
    x_blocks = projected[:, :hp_width].reshape(block_count, block_len, head_count, head_dim)
    b_blocks = projected[:, hp_width : hp_width + state_width].reshape(
        block_count, block_len, state_width
    )
    c_blocks = projected[:, hp_width + state_width :].reshape(block_count, block_len, state_width)
    g_blocks = grad_out.reshape(block_count, block_len, head_count, head_dim)
    ld_blocks = log_decay[0].reshape(head_count, block_count, block_len).transpose(1, 0, 2)
    decays, fwd_states, back_states = jax.vmap(summaries)(
        x_blocks, b_blocks, c_blocks, g_blocks, ld_blocks
    )
    zero_state = jnp.zeros((head_count, state_width, head_dim), jnp.float32)
    dev_decay = jnp.prod(decays, axis=0)
    dev_fwd, unused_a = state_chain(decays, fwd_states, zero_state, False)
    dev_back, unused_b = state_chain(decays, back_states, zero_state, True)
    carried = (None, scan_entering(dev_decay, dev_fwd, "seq", False))
    returned = (None, scan_entering(dev_decay, dev_back, "seq", True))
    unused_c, state_starts = state_chain(decays, fwd_states, carried[1], False)
    unused_d, back_starts = state_chain(decays, back_states, returned[1], True)
    d_x, d_b, d_c = lax.map(
        lambda block_item: block_grads(*block_item),
        (x_blocks, b_blocks, c_blocks, g_blocks, ld_blocks, state_starts, back_starts),
    )
    d_proj = jnp.concatenate(
        [
            d_x.reshape(tok_count, hp_width),
            d_b.reshape(tok_count, state_width),
            d_c.reshape(tok_count, state_width),
        ],
        axis=1,
    ).astype(jnp.bfloat16)
    grad_in = lax.dot_general(
        d_proj, weights, (((1,), (1,)), ((), ())), preferred_element_type=jnp.float32
    )
    seq_count = lax.axis_size("seq")
    group_count = lax.axis_size("dp")
    norm_factor = 1.0 / math.sqrt(group_count * seq_count * tok_count)
    partial_grad = seq_reduce_scatter(
        outer_product(features, d_proj),
        "seq",
    )
    summed_grad = replicated_sum(partial_grad, "dp")
    return (grad_in[None], summed_grad * norm_factor)


def solution(mesh):
    placed = (
        P("dp", "seq", None),
        P("seq", None),
        P("seq", None),
        P("dp", None, "seq"),
        P("dp", "seq", None),
    )
    return jax.shard_map(
        local,
        mesh=mesh,
        in_specs=placed,
        out_specs=(P("dp", "seq", None), P("seq", None)),
        check_vma=False,
    )
```

```python
import math

import jax
import jax.numpy as jnp
from jax import lax
from jax.sharding import PartitionSpec as P
from jax.experimental import pallas as pl
from jax.experimental.pallas import tpu as pltpu


def shifted(value, axis, step, reverse):
    count = lax.axis_size(axis)
    if reverse:
        pairs = [(place, place - step) for place in range(step, count)]
    else:
        pairs = [(place, place + step) for place in range(count - step)]
    return lax.ppermute(value.astype(jnp.bfloat16), axis, pairs).astype(value.dtype)


def scan_entering(decay, state, axis, reverse):
    head_count = state.shape[0]
    flat = state.reshape(head_count, -1)
    split = flat.shape[1]
    count = lax.axis_size(axis)

    def send(part, step):
        flat, decay = part
        high = lax.reduce_precision(decay, exponent_bits=8, mantissa_bits=7)
        lanes = lambda piece: jnp.broadcast_to(piece[:, None], (head_count, 128))
        packed = jnp.concatenate([flat, lanes(high), lanes(decay - high)], axis=1)
        got = shifted(packed, axis, step, reverse)
        return got[:, :split], got[:, split] + got[:, split + 128]

    def chain(parts):
        flat, decay = parts[0]
        for later_flat, later_decay in parts[1:]:
            flat = later_decay[:, None] * flat + later_flat
            decay = decay * later_decay
        return flat, decay

    radix = 2
    own = (flat, decay)
    part = chain([send(own, step) for step in range(radix, 0, -1)])
    width = radix
    while width < count:
        pieces = min(radix, -(-count // width))
        part = chain([send(part, width * m) for m in range(pieces - 1, 0, -1)] + [part])
        width *= pieces
    flat = part[0]
    return flat.reshape(state.shape)


def butterfly_sum(value, axis):
    count = lax.axis_size(axis)
    step = 1
    while step < count:
        pairs = [(place, place ^ step) for place in range(count)]
        value = value + lax.ppermute(value, axis, pairs)
        step *= 2
    return value


def digit_reduce(value, axis, where, stride, radix):
    count = lax.axis_size(axis)
    digit = (lax.axis_index(axis) // stride) % radix
    total = lax.dynamic_index_in_dim(value, digit, where, False).astype(jnp.float32)
    for offset in range(1, radix):
        piece = lax.dynamic_index_in_dim(value, (digit + offset) % radix, where, False)
        pairs = [
            (place, place + (((place // stride) % radix + offset) % radix - (place // stride) % radix) * stride)
            for place in range(count)
        ]
        got = lax.ppermute(piece.astype(jnp.bfloat16), axis, pairs)
        total = total + got.astype(jnp.float32)
    return total


def seq_reduce_scatter(partial, axis):
    rows, cols = partial.shape
    count = lax.axis_size(axis)
    block = rows // count
    value = partial.reshape(count // 8, 4, 2, block, cols)
    value = digit_reduce(value, axis, 2, 1, 2)
    half = cols // 2
    first = digit_reduce(value[..., :half], axis, 1, 2, 4)
    first = digit_reduce(first, axis, 0, 8, count // 8)
    second = digit_reduce(value[..., half:], axis, 0, 8, count // 8)
    second = digit_reduce(second, axis, 0, 2, 4)
    return jnp.concatenate([first, second], axis=1)


def replicated_sum(value, axis):
    count = lax.axis_size(axis)
    me = lax.axis_index(axis)
    steps = []
    step = count // 2
    while step >= 1:
        steps.append(step)
        step //= 2
    total = value
    for step in steps:
        pairs = [(place, place ^ step) for place in range(count)]
        halves = total.reshape(2, total.shape[0] // 2, total.shape[1])
        bit = (me // step) % 2
        keep = lax.dynamic_index_in_dim(halves, bit, 0, False)
        give = lax.dynamic_index_in_dim(halves, 1 - bit, 0, False)
        total = keep + lax.ppermute(give, axis, pairs)
    for step in reversed(steps):
        pairs = [(place, place ^ step) for place in range(count)]
        other = lax.ppermute(total, axis, pairs)
        bit = (me // step) % 2
        total = jnp.where(
            bit == 0,
            jnp.concatenate([total, other], axis=0),
            jnp.concatenate([other, total], axis=0),
        )
    return total


def outer_kernel(left_ref, right_ref, out_ref):
    out_ref[...] = lax.dot_general(
        left_ref[...], right_ref[...], (((0,), (0,)), ((), ())), preferred_element_type=jnp.float32
    ).astype(out_ref.dtype)


def outer_product(left, right):
    depth, rows = left.shape
    cols = right.shape[1]
    tile = 256
    return pl.pallas_call(
        outer_kernel,
        grid=(rows // tile,),
        in_specs=[
            pl.BlockSpec((depth, tile), lambda i: (0, i)),
            pl.BlockSpec((depth, cols), lambda i: (0, 0)),
        ],
        out_specs=pl.BlockSpec((tile, cols), lambda i: (i, 0)),
        out_shape=jax.ShapeDtypeStruct((rows, cols), jnp.bfloat16),
        cost_estimate=pl.CostEstimate(
            flops=2 * depth * rows * cols,
            bytes_accessed=2 * (depth * rows + depth * cols + rows * cols),
            transcendentals=0,
        ),
    )(left, right)


def dequantize(code_rows, scale_rows):
    row_count, col_count = code_rows.shape
    group_count = scale_rows.shape[1]
    spread = code_rows.astype(jnp.float32).reshape(row_count, group_count, col_count // group_count)
    spread = spread * scale_rows.astype(jnp.float32)[:, :, None]
    return spread.reshape(row_count, col_count).astype(jnp.bfloat16)


def block_prep(ld_block):
    cum_log = jnp.cumsum(ld_block, axis=1)
    input_scale = jnp.sqrt(-jnp.expm1(2.0 * ld_block))
    tail_weight = jnp.exp(cum_log[:, -1:] - cum_log) * input_scale
    return (cum_log, input_scale, tail_weight)


def weighted_pair(x_vals, grad_out, tail_weight, cum_log, inv_root):
    head_weight = jnp.exp(cum_log) * inv_root
    weighted_x = (x_vals.astype(jnp.float32) * tail_weight.T[:, :, None]).astype(jnp.bfloat16)
    weighted_g = (grad_out.astype(jnp.float32) * head_weight.T[:, :, None]).astype(jnp.bfloat16)
    return (weighted_x, weighted_g)


def summaries(x_vals, b_mat, c_mat, grad_out, ld_block):
    cum_log, input_scale, tail_weight = block_prep(ld_block)
    inv_root = 1.0 / math.sqrt(b_mat.shape[1])
    weighted_x, weighted_g = weighted_pair(x_vals, grad_out, tail_weight, cum_log, inv_root)
    fwd_state = jnp.einsum("sn,shp->hnp", b_mat, weighted_x, preferred_element_type=jnp.float32)
    back_state = jnp.einsum("tn,thp->hnp", c_mat, weighted_g, preferred_element_type=jnp.float32)
    return (jnp.exp(cum_log[:, -1]), fwd_state, back_state)


def block_grads(x_vals, b_mat, c_mat, grad_out, ld_block, state_in, back_in):
    block_len = ld_block.shape[1]
    cum_log, input_scale, tail_weight = block_prep(ld_block)
    inv_root = 1.0 / math.sqrt(b_mat.shape[1])
    weighted_x, weighted_g = weighted_pair(x_vals, grad_out, tail_weight, cum_log, inv_root)
    row_ids = lax.broadcasted_iota(jnp.int32, (block_len, block_len), 0)
    col_ids = lax.broadcasted_iota(jnp.int32, (block_len, block_len), 1)
    lower_mask = (row_ids >= col_ids)[None]
    log_gap = cum_log[:, :, None] - cum_log[:, None, :]
    decay_mat = jnp.where(lower_mask, jnp.exp(jnp.where(lower_mask, log_gap, 0.0)), 0.0)
    state_low = state_in.astype(jnp.bfloat16)
    back_low = back_in.astype(jnp.bfloat16)
    x_dot_g = jnp.einsum("thp,shp->hts", grad_out, x_vals, preferred_element_type=jnp.float32)
    c_dot_b = jnp.dot(c_mat, b_mat.T, preferred_element_type=jnp.float32)
    mix_weights = (
        jnp.sum(decay_mat * input_scale[:, None, :] * x_dot_g, axis=0) * inv_root
    ).astype(jnp.bfloat16)
    d_c = jnp.einsum("hnp,thp->tn", state_low, weighted_g, preferred_element_type=jnp.float32)
    d_c = d_c + jnp.dot(mix_weights, b_mat, preferred_element_type=jnp.float32)
    d_b = jnp.einsum("hnp,thp->tn", back_low, weighted_x, preferred_element_type=jnp.float32)
    d_b = d_b + jnp.dot(mix_weights.T, c_mat, preferred_element_type=jnp.float32)
    d_x = (
        jnp.einsum("tn,hnp->thp", b_mat, back_low, preferred_element_type=jnp.float32)
        * tail_weight.T[:, :, None]
    )
    inner_weights = (decay_mat * c_dot_b[None] * inv_root).astype(jnp.bfloat16)
    inner = jnp.einsum("hus,uhp->shp", inner_weights, grad_out, preferred_element_type=jnp.float32)
    d_x = d_x + input_scale.T[:, :, None] * inner
    return (d_x, d_b, d_c)


def state_chain(decays, adds, start, backward):

    def step(carry, item):
        return (item[0][:, None, None] * carry + item[1], carry)

    return lax.scan(step, start, (decays, adds), reverse=backward)


def local(inputs, weight_codes, scales, log_decay, cotangent):
    tok_count = inputs.shape[1]
    features = inputs[0]
    grad_out = cotangent[0]
    head_count = log_decay.shape[1]
    hp_width = grad_out.shape[1]
    head_dim = hp_width // head_count
    proj_width = weight_codes.shape[1]
    state_width = (proj_width - hp_width) // 2
    weights = lax.all_gather(dequantize(weight_codes, scales), "seq", axis=0, tiled=True)
    projected = jnp.dot(features, weights, preferred_element_type=jnp.float32).astype(jnp.bfloat16)
    block_len = min(128, tok_count)
    block_count = tok_count // block_len
    x_blocks = projected[:, :hp_width].reshape(block_count, block_len, head_count, head_dim)
    b_blocks = projected[:, hp_width : hp_width + state_width].reshape(
        block_count, block_len, state_width
    )
    c_blocks = projected[:, hp_width + state_width :].reshape(block_count, block_len, state_width)
    g_blocks = grad_out.reshape(block_count, block_len, head_count, head_dim)
    ld_blocks = log_decay[0].reshape(head_count, block_count, block_len).transpose(1, 0, 2)
    decays, fwd_states, back_states = jax.vmap(summaries)(
        x_blocks, b_blocks, c_blocks, g_blocks, ld_blocks
    )
    zero_state = jnp.zeros((head_count, state_width, head_dim), jnp.float32)
    dev_decay = jnp.prod(decays, axis=0)
    dev_fwd, unused_a = state_chain(decays, fwd_states, zero_state, False)
    dev_back, unused_b = state_chain(decays, back_states, zero_state, True)
    carried = (None, scan_entering(dev_decay, dev_fwd, "seq", False))
    returned = (None, scan_entering(dev_decay, dev_back, "seq", True))
    unused_c, state_starts = state_chain(decays, fwd_states, carried[1], False)
    unused_d, back_starts = state_chain(decays, back_states, returned[1], True)
    d_x, d_b, d_c = lax.map(
        lambda block_item: block_grads(*block_item),
        (x_blocks, b_blocks, c_blocks, g_blocks, ld_blocks, state_starts, back_starts),
    )
    d_proj = jnp.concatenate(
        [
            d_x.reshape(tok_count, hp_width),
            d_b.reshape(tok_count, state_width),
            d_c.reshape(tok_count, state_width),
        ],
        axis=1,
    ).astype(jnp.bfloat16)
    grad_in = lax.dot_general(
        d_proj, weights, (((1,), (1,)), ((), ())), preferred_element_type=jnp.float32
    )
    seq_count = lax.axis_size("seq")
    group_count = lax.axis_size("dp")
    norm_factor = 1.0 / math.sqrt(group_count * seq_count * tok_count)
    partial_grad = seq_reduce_scatter(
        outer_product(features, d_proj),
        "seq",
    )
    summed_grad = replicated_sum(partial_grad, "dp")
    return (grad_in[None], summed_grad * norm_factor)


def solution(mesh):
    placed = (
        P("dp", "seq", None),
        P("seq", None),
        P("seq", None),
        P("dp", None, "seq"),
        P("dp", "seq", None),
    )
    return jax.shard_map(
        local,
        mesh=mesh,
        in_specs=placed,
        out_specs=(P("dp", "seq", None), P("seq", None)),
        check_vma=False,
    )
```

```python
import math

import jax
import jax.numpy as jnp
from jax import lax
from jax.sharding import PartitionSpec as P
from jax.experimental import pallas as pl
from jax.experimental.pallas import tpu as pltpu


def shifted(value, axis, step, reverse):
    count = lax.axis_size(axis)
    if reverse:
        pairs = [(place, place - step) for place in range(step, count)]
    else:
        pairs = [(place, place + step) for place in range(count - step)]
    return lax.ppermute(value.astype(jnp.bfloat16), axis, pairs).astype(value.dtype)


def scan_entering(decay, state, axis, reverse):
    head_count = state.shape[0]
    flat = state.reshape(head_count, -1)
    split = flat.shape[1]
    count = lax.axis_size(axis)

    def send(part, step):
        flat, decay = part
        high = lax.reduce_precision(decay, exponent_bits=8, mantissa_bits=7)
        lanes = lambda piece: jnp.broadcast_to(piece[:, None], (head_count, 128))
        packed = jnp.concatenate([flat, lanes(high), lanes(decay - high)], axis=1)
        got = shifted(packed, axis, step, reverse)
        return got[:, :split], got[:, split] + got[:, split + 128]

    def chain(parts):
        flat, decay = parts[0]
        for later_flat, later_decay in parts[1:]:
            flat = later_decay[:, None] * flat + later_flat
            decay = decay * later_decay
        return flat, decay

    radix = 2
    own = (flat, decay)
    part = chain([send(own, step) for step in range(radix, 0, -1)])
    width = radix
    while width < count:
        pieces = min(radix, -(-count // width))
        part = chain([send(part, width * m) for m in range(pieces - 1, 0, -1)] + [part])
        width *= pieces
    flat = part[0]
    return flat.reshape(state.shape)


def butterfly_sum(value, axis):
    count = lax.axis_size(axis)
    step = 1
    while step < count:
        pairs = [(place, place ^ step) for place in range(count)]
        value = value + lax.ppermute(value, axis, pairs)
        step *= 2
    return value


def digit_reduce(value, axis, where, stride, radix):
    count = lax.axis_size(axis)
    digit = (lax.axis_index(axis) // stride) % radix
    total = lax.dynamic_index_in_dim(value, digit, where, False).astype(jnp.float32)
    for offset in range(1, radix):
        piece = lax.dynamic_index_in_dim(value, (digit + offset) % radix, where, False)
        pairs = [
            (place, place + (((place // stride) % radix + offset) % radix - (place // stride) % radix) * stride)
            for place in range(count)
        ]
        got = lax.ppermute(piece.astype(jnp.bfloat16), axis, pairs)
        total = total + got.astype(jnp.float32)
    return total


def seq_reduce_scatter(partial, axis):
    rows, cols = partial.shape
    count = lax.axis_size(axis)
    block = rows // count
    value = partial.reshape(count // 8, 4, 2, block, cols)
    value = digit_reduce(value, axis, 2, 1, 2)
    half = cols // 2
    first = digit_reduce(value[..., :half], axis, 1, 2, 4)
    first = digit_reduce(first, axis, 0, 8, count // 8)
    second = digit_reduce(value[..., half:], axis, 0, 8, count // 8)
    second = digit_reduce(second, axis, 0, 2, 4)
    return jnp.concatenate([first, second], axis=1)


def replicated_sum(value, axis):
    count = lax.axis_size(axis)
    me = lax.axis_index(axis)
    slabs = value.reshape(count, value.shape[0] // count, value.shape[1])
    total = lax.dynamic_index_in_dim(slabs, me, 0, False)
    for offset in range(1, count):
        piece = lax.dynamic_index_in_dim(slabs, (me + offset) % count, 0, False)
        pairs = [(place, (place + offset) % count) for place in range(count)]
        total = total + lax.ppermute(piece, axis, pairs)
    gathered = [total]
    for offset in range(1, count):
        pairs = [(place, (place + offset) % count) for place in range(count)]
        gathered.append(lax.ppermute(total, axis, pairs))
    stacked = jnp.stack(gathered)
    order = (me - jnp.arange(count)) % count
    return jnp.take(stacked, order, axis=0).reshape(value.shape)


def outer_kernel(left_ref, right_ref, out_ref):
    out_ref[...] = jnp.dot(
        left_ref[...], right_ref[...], preferred_element_type=jnp.float32
    ).astype(out_ref.dtype)


def outer_product(left, right):
    depth, rows = left.shape
    cols = right.shape[1]
    tile = 512
    return pl.pallas_call(
        outer_kernel,
        grid=(rows // tile,),
        in_specs=[
            pl.BlockSpec((tile, depth), lambda i: (i, 0)),
            pl.BlockSpec((depth, cols), lambda i: (0, 0)),
        ],
        out_specs=pl.BlockSpec((tile, cols), lambda i: (i, 0)),
        out_shape=jax.ShapeDtypeStruct((rows, cols), jnp.bfloat16),
        cost_estimate=pl.CostEstimate(
            flops=2 * depth * rows * cols,
            bytes_accessed=2 * (depth * rows + depth * cols + rows * cols),
            transcendentals=0,
        ),
    )(left.T, right)


def dequantize(code_rows, scale_rows):
    row_count, col_count = code_rows.shape
    group_count = scale_rows.shape[1]
    spread = code_rows.astype(jnp.float32).reshape(row_count, group_count, col_count // group_count)
    spread = spread * scale_rows.astype(jnp.float32)[:, :, None]
    return spread.reshape(row_count, col_count).astype(jnp.bfloat16)


def block_prep(ld_block):
    cum_log = jnp.cumsum(ld_block, axis=1)
    input_scale = jnp.sqrt(-jnp.expm1(2.0 * ld_block))
    tail_weight = jnp.exp(cum_log[:, -1:] - cum_log) * input_scale
    return (cum_log, input_scale, tail_weight)


def weighted_pair(x_vals, grad_out, tail_weight, cum_log, inv_root):
    head_weight = jnp.exp(cum_log) * inv_root
    weighted_x = (x_vals.astype(jnp.float32) * tail_weight.T[:, :, None]).astype(jnp.bfloat16)
    weighted_g = (grad_out.astype(jnp.float32) * head_weight.T[:, :, None]).astype(jnp.bfloat16)
    return (weighted_x, weighted_g)


def summaries(x_vals, b_mat, c_mat, grad_out, ld_block):
    cum_log, input_scale, tail_weight = block_prep(ld_block)
    inv_root = 1.0 / math.sqrt(b_mat.shape[1])
    weighted_x, weighted_g = weighted_pair(x_vals, grad_out, tail_weight, cum_log, inv_root)
    fwd_state = jnp.einsum("sn,shp->hnp", b_mat, weighted_x, preferred_element_type=jnp.float32)
    back_state = jnp.einsum("tn,thp->hnp", c_mat, weighted_g, preferred_element_type=jnp.float32)
    return (jnp.exp(cum_log[:, -1]), fwd_state, back_state)


def block_grads(x_vals, b_mat, c_mat, grad_out, ld_block, state_in, back_in):
    block_len = ld_block.shape[1]
    cum_log, input_scale, tail_weight = block_prep(ld_block)
    inv_root = 1.0 / math.sqrt(b_mat.shape[1])
    weighted_x, weighted_g = weighted_pair(x_vals, grad_out, tail_weight, cum_log, inv_root)
    row_ids = lax.broadcasted_iota(jnp.int32, (block_len, block_len), 0)
    col_ids = lax.broadcasted_iota(jnp.int32, (block_len, block_len), 1)
    lower_mask = (row_ids >= col_ids)[None]
    log_gap = cum_log[:, :, None] - cum_log[:, None, :]
    decay_mat = jnp.where(lower_mask, jnp.exp(jnp.where(lower_mask, log_gap, 0.0)), 0.0)
    state_low = state_in.astype(jnp.bfloat16)
    back_low = back_in.astype(jnp.bfloat16)
    x_dot_g = jnp.einsum("thp,shp->hts", grad_out, x_vals, preferred_element_type=jnp.float32)
    c_dot_b = jnp.dot(c_mat, b_mat.T, preferred_element_type=jnp.float32)
    mix_weights = (
        jnp.sum(decay_mat * input_scale[:, None, :] * x_dot_g, axis=0) * inv_root
    ).astype(jnp.bfloat16)
    d_c = jnp.einsum("hnp,thp->tn", state_low, weighted_g, preferred_element_type=jnp.float32)
    d_c = d_c + jnp.dot(mix_weights, b_mat, preferred_element_type=jnp.float32)
    d_b = jnp.einsum("hnp,thp->tn", back_low, weighted_x, preferred_element_type=jnp.float32)
    d_b = d_b + jnp.dot(mix_weights.T, c_mat, preferred_element_type=jnp.float32)
    d_x = (
        jnp.einsum("tn,hnp->thp", b_mat, back_low, preferred_element_type=jnp.float32)
        * tail_weight.T[:, :, None]
    )
    inner_weights = (decay_mat * c_dot_b[None] * inv_root).astype(jnp.bfloat16)
    inner = jnp.einsum("hus,uhp->shp", inner_weights, grad_out, preferred_element_type=jnp.float32)
    d_x = d_x + input_scale.T[:, :, None] * inner
    return (d_x, d_b, d_c)


def state_chain(decays, adds, start, backward):

    def step(carry, item):
        return (item[0][:, None, None] * carry + item[1], carry)

    return lax.scan(step, start, (decays, adds), reverse=backward)


def local(inputs, weight_codes, scales, log_decay, cotangent):
    tok_count = inputs.shape[1]
    features = inputs[0]
    grad_out = cotangent[0]
    head_count = log_decay.shape[1]
    hp_width = grad_out.shape[1]
    head_dim = hp_width // head_count
    proj_width = weight_codes.shape[1]
    state_width = (proj_width - hp_width) // 2
    weights = lax.all_gather(dequantize(weight_codes, scales), "seq", axis=0, tiled=True)
    projected = jnp.dot(features, weights, preferred_element_type=jnp.float32).astype(jnp.bfloat16)
    block_len = min(128, tok_count)
    block_count = tok_count // block_len
    x_blocks = projected[:, :hp_width].reshape(block_count, block_len, head_count, head_dim)
    b_blocks = projected[:, hp_width : hp_width + state_width].reshape(
        block_count, block_len, state_width
    )
    c_blocks = projected[:, hp_width + state_width :].reshape(block_count, block_len, state_width)
    g_blocks = grad_out.reshape(block_count, block_len, head_count, head_dim)
    ld_blocks = log_decay[0].reshape(head_count, block_count, block_len).transpose(1, 0, 2)
    decays, fwd_states, back_states = jax.vmap(summaries)(
        x_blocks, b_blocks, c_blocks, g_blocks, ld_blocks
    )
    zero_state = jnp.zeros((head_count, state_width, head_dim), jnp.float32)
    dev_decay = jnp.prod(decays, axis=0)
    dev_fwd, unused_a = state_chain(decays, fwd_states, zero_state, False)
    dev_back, unused_b = state_chain(decays, back_states, zero_state, True)
    carried = (None, scan_entering(dev_decay, dev_fwd, "seq", False))
    returned = (None, scan_entering(dev_decay, dev_back, "seq", True))
    unused_c, state_starts = state_chain(decays, fwd_states, carried[1], False)
    unused_d, back_starts = state_chain(decays, back_states, returned[1], True)
    d_x, d_b, d_c = lax.map(
        lambda block_item: block_grads(*block_item),
        (x_blocks, b_blocks, c_blocks, g_blocks, ld_blocks, state_starts, back_starts),
    )
    d_proj = jnp.concatenate(
        [
            d_x.reshape(tok_count, hp_width),
            d_b.reshape(tok_count, state_width),
            d_c.reshape(tok_count, state_width),
        ],
        axis=1,
    ).astype(jnp.bfloat16)
    grad_in = lax.dot_general(
        d_proj, weights, (((1,), (1,)), ((), ())), preferred_element_type=jnp.float32
    )
    seq_count = lax.axis_size("seq")
    group_count = lax.axis_size("dp")
    norm_factor = 1.0 / math.sqrt(group_count * seq_count * tok_count)
    partial_grad = seq_reduce_scatter(
        outer_product(features, d_proj),
        "seq",
    )
    summed_grad = replicated_sum(partial_grad, "dp")
    return (grad_in[None], summed_grad * norm_factor)


def solution(mesh):
    placed = (
        P("dp", "seq", None),
        P("seq", None),
        P("seq", None),
        P("dp", None, "seq"),
        P("dp", "seq", None),
    )
    return jax.shard_map(
        local,
        mesh=mesh,
        in_specs=placed,
        out_specs=(P("dp", "seq", None), P("seq", None)),
        check_vma=False,
    )
```

```python
import math

import jax
import jax.numpy as jnp
from jax import lax
from jax.sharding import PartitionSpec as P
from jax.experimental import pallas as pl
from jax.experimental.pallas import tpu as pltpu


def shifted(value, axis, step, reverse):
    count = lax.axis_size(axis)
    if reverse:
        pairs = [(place, place - step) for place in range(step, count)]
    else:
        pairs = [(place, place + step) for place in range(count - step)]
    return lax.ppermute(value.astype(jnp.bfloat16), axis, pairs).astype(value.dtype)


def scan_entering(decay, state, axis, reverse):
    head_count = state.shape[0]
    flat = state.reshape(head_count, -1)
    split = flat.shape[1]
    count = lax.axis_size(axis)

    def send(part, step):
        flat, decay = part
        high = lax.reduce_precision(decay, exponent_bits=8, mantissa_bits=7)
        lanes = lambda piece: jnp.broadcast_to(piece[:, None], (head_count, 128))
        packed = jnp.concatenate([flat, lanes(high), lanes(decay - high)], axis=1)
        got = shifted(packed, axis, step, reverse)
        return got[:, :split], got[:, split] + got[:, split + 128]

    def chain(parts):
        flat, decay = parts[0]
        for later_flat, later_decay in parts[1:]:
            flat = later_decay[:, None] * flat + later_flat
            decay = decay * later_decay
        return flat, decay

    radix = 2
    own = (flat, decay)
    part = chain([send(own, step) for step in range(radix, 0, -1)])
    width = radix
    while width < count:
        pieces = min(radix, -(-count // width))
        part = chain([send(part, width * m) for m in range(pieces - 1, 0, -1)] + [part])
        width *= pieces
    flat = part[0]
    return flat.reshape(state.shape)


def butterfly_sum(value, axis):
    count = lax.axis_size(axis)
    step = 1
    while step < count:
        pairs = [(place, place ^ step) for place in range(count)]
        value = value + lax.ppermute(value, axis, pairs)
        step *= 2
    return value


def digit_reduce(value, axis, where, stride, radix):
    count = lax.axis_size(axis)
    digit = (lax.axis_index(axis) // stride) % radix
    total = lax.dynamic_index_in_dim(value, digit, where, False).astype(jnp.float32)
    for offset in range(1, radix):
        piece = lax.dynamic_index_in_dim(value, (digit + offset) % radix, where, False)
        pairs = [
            (place, place + (((place // stride) % radix + offset) % radix - (place // stride) % radix) * stride)
            for place in range(count)
        ]
        got = lax.ppermute(piece.astype(jnp.bfloat16), axis, pairs)
        total = total + got.astype(jnp.float32)
    return total


def seq_reduce_scatter(partial, axis):
    rows, cols = partial.shape
    count = lax.axis_size(axis)
    block = rows // count
    value = partial.reshape(count // 8, 4, 2, block, cols)
    value = digit_reduce(value, axis, 2, 1, 2)
    value = digit_reduce(value, axis, 1, 2, 4)
    return digit_reduce(value, axis, 0, 8, count // 8)


def replicated_sum(value, axis):
    count = lax.axis_size(axis)
    me = lax.axis_index(axis)
    slabs = value.reshape(count, value.shape[0] // count, value.shape[1])
    total = lax.dynamic_index_in_dim(slabs, me, 0, False)
    for offset in range(1, count):
        piece = lax.dynamic_index_in_dim(slabs, (me + offset) % count, 0, False)
        pairs = [(place, (place + offset) % count) for place in range(count)]
        total = total + lax.ppermute(piece, axis, pairs)
    gathered = [total]
    for offset in range(1, count):
        pairs = [(place, (place + offset) % count) for place in range(count)]
        gathered.append(lax.ppermute(total, axis, pairs))
    stacked = jnp.stack(gathered)
    order = (me - jnp.arange(count)) % count
    return jnp.take(stacked, order, axis=0).reshape(value.shape)


def outer_kernel(left_ref, right_ref, out_ref):
    out_ref[...] = jnp.dot(
        left_ref[...], right_ref[...], preferred_element_type=jnp.float32
    ).astype(out_ref.dtype)


def outer_product(left, right):
    depth, rows = left.shape
    cols = right.shape[1]
    tile = 1024
    return pl.pallas_call(
        outer_kernel,
        grid=(rows // tile,),
        in_specs=[
            pl.BlockSpec((tile, depth), lambda i: (i, 0)),
            pl.BlockSpec((depth, cols), lambda i: (0, 0)),
        ],
        out_specs=pl.BlockSpec((tile, cols), lambda i: (i, 0)),
        out_shape=jax.ShapeDtypeStruct((rows, cols), jnp.bfloat16),
        cost_estimate=pl.CostEstimate(
            flops=2 * depth * rows * cols,
            bytes_accessed=2 * (depth * rows + depth * cols + rows * cols),
            transcendentals=0,
        ),
    )(left.T, right)


def dequantize(code_rows, scale_rows):
    row_count, col_count = code_rows.shape
    group_count = scale_rows.shape[1]
    spread = code_rows.astype(jnp.float32).reshape(row_count, group_count, col_count // group_count)
    spread = spread * scale_rows.astype(jnp.float32)[:, :, None]
    return spread.reshape(row_count, col_count).astype(jnp.bfloat16)


def block_prep(ld_block):
    cum_log = jnp.cumsum(ld_block, axis=1)
    input_scale = jnp.sqrt(-jnp.expm1(2.0 * ld_block))
    tail_weight = jnp.exp(cum_log[:, -1:] - cum_log) * input_scale
    return (cum_log, input_scale, tail_weight)


def weighted_pair(x_vals, grad_out, tail_weight, cum_log, inv_root):
    head_weight = jnp.exp(cum_log) * inv_root
    weighted_x = (x_vals.astype(jnp.float32) * tail_weight.T[:, :, None]).astype(jnp.bfloat16)
    weighted_g = (grad_out.astype(jnp.float32) * head_weight.T[:, :, None]).astype(jnp.bfloat16)
    return (weighted_x, weighted_g)


def summaries(x_vals, b_mat, c_mat, grad_out, ld_block):
    cum_log, input_scale, tail_weight = block_prep(ld_block)
    inv_root = 1.0 / math.sqrt(b_mat.shape[1])
    weighted_x, weighted_g = weighted_pair(x_vals, grad_out, tail_weight, cum_log, inv_root)
    fwd_state = jnp.einsum("sn,shp->hnp", b_mat, weighted_x, preferred_element_type=jnp.float32)
    back_state = jnp.einsum("tn,thp->hnp", c_mat, weighted_g, preferred_element_type=jnp.float32)
    return (jnp.exp(cum_log[:, -1]), fwd_state, back_state)


def block_grads(x_vals, b_mat, c_mat, grad_out, ld_block, state_in, back_in):
    block_len = ld_block.shape[1]
    cum_log, input_scale, tail_weight = block_prep(ld_block)
    inv_root = 1.0 / math.sqrt(b_mat.shape[1])
    weighted_x, weighted_g = weighted_pair(x_vals, grad_out, tail_weight, cum_log, inv_root)
    row_ids = lax.broadcasted_iota(jnp.int32, (block_len, block_len), 0)
    col_ids = lax.broadcasted_iota(jnp.int32, (block_len, block_len), 1)
    lower_mask = (row_ids >= col_ids)[None]
    log_gap = cum_log[:, :, None] - cum_log[:, None, :]
    decay_mat = jnp.where(lower_mask, jnp.exp(jnp.where(lower_mask, log_gap, 0.0)), 0.0)
    state_low = state_in.astype(jnp.bfloat16)
    back_low = back_in.astype(jnp.bfloat16)
    x_dot_g = jnp.einsum("thp,shp->hts", grad_out, x_vals, preferred_element_type=jnp.float32)
    c_dot_b = jnp.dot(c_mat, b_mat.T, preferred_element_type=jnp.float32)
    mix_weights = (
        jnp.sum(decay_mat * input_scale[:, None, :] * x_dot_g, axis=0) * inv_root
    ).astype(jnp.bfloat16)
    d_c = jnp.einsum("hnp,thp->tn", state_low, weighted_g, preferred_element_type=jnp.float32)
    d_c = d_c + jnp.dot(mix_weights, b_mat, preferred_element_type=jnp.float32)
    d_b = jnp.einsum("hnp,thp->tn", back_low, weighted_x, preferred_element_type=jnp.float32)
    d_b = d_b + jnp.dot(mix_weights.T, c_mat, preferred_element_type=jnp.float32)
    d_x = (
        jnp.einsum("tn,hnp->thp", b_mat, back_low, preferred_element_type=jnp.float32)
        * tail_weight.T[:, :, None]
    )
    inner_weights = (decay_mat * c_dot_b[None] * inv_root).astype(jnp.bfloat16)
    inner = jnp.einsum("hus,uhp->shp", inner_weights, grad_out, preferred_element_type=jnp.float32)
    d_x = d_x + input_scale.T[:, :, None] * inner
    return (d_x, d_b, d_c)


def state_chain(decays, adds, start, backward):

    def step(carry, item):
        return (item[0][:, None, None] * carry + item[1], carry)

    return lax.scan(step, start, (decays, adds), reverse=backward)


def local(inputs, weight_codes, scales, log_decay, cotangent):
    tok_count = inputs.shape[1]
    features = inputs[0]
    grad_out = cotangent[0]
    head_count = log_decay.shape[1]
    hp_width = grad_out.shape[1]
    head_dim = hp_width // head_count
    proj_width = weight_codes.shape[1]
    state_width = (proj_width - hp_width) // 2
    weights = lax.all_gather(dequantize(weight_codes, scales), "seq", axis=0, tiled=True)
    projected = jnp.dot(features, weights, preferred_element_type=jnp.float32).astype(jnp.bfloat16)
    block_len = min(128, tok_count)
    block_count = tok_count // block_len
    x_blocks = projected[:, :hp_width].reshape(block_count, block_len, head_count, head_dim)
    b_blocks = projected[:, hp_width : hp_width + state_width].reshape(
        block_count, block_len, state_width
    )
    c_blocks = projected[:, hp_width + state_width :].reshape(block_count, block_len, state_width)
    g_blocks = grad_out.reshape(block_count, block_len, head_count, head_dim)
    ld_blocks = log_decay[0].reshape(head_count, block_count, block_len).transpose(1, 0, 2)
    decays, fwd_states, back_states = jax.vmap(summaries)(
        x_blocks, b_blocks, c_blocks, g_blocks, ld_blocks
    )
    zero_state = jnp.zeros((head_count, state_width, head_dim), jnp.float32)
    dev_decay = jnp.prod(decays, axis=0)
    dev_fwd, unused_a = state_chain(decays, fwd_states, zero_state, False)
    dev_back, unused_b = state_chain(decays, back_states, zero_state, True)
    carried = (None, scan_entering(dev_decay, dev_fwd, "seq", False))
    returned = (None, scan_entering(dev_decay, dev_back, "seq", True))
    unused_c, state_starts = state_chain(decays, fwd_states, carried[1], False)
    unused_d, back_starts = state_chain(decays, back_states, returned[1], True)
    d_x, d_b, d_c = lax.map(
        lambda block_item: block_grads(*block_item),
        (x_blocks, b_blocks, c_blocks, g_blocks, ld_blocks, state_starts, back_starts),
    )
    d_proj = jnp.concatenate(
        [
            d_x.reshape(tok_count, hp_width),
            d_b.reshape(tok_count, state_width),
            d_c.reshape(tok_count, state_width),
        ],
        axis=1,
    ).astype(jnp.bfloat16)
    grad_in = lax.dot_general(
        d_proj, weights, (((1,), (1,)), ((), ())), preferred_element_type=jnp.float32
    )
    seq_count = lax.axis_size("seq")
    group_count = lax.axis_size("dp")
    norm_factor = 1.0 / math.sqrt(group_count * seq_count * tok_count)
    partial_grad = seq_reduce_scatter(
        outer_product(features, d_proj),
        "seq",
    )
    summed_grad = replicated_sum(partial_grad, "dp")
    return (grad_in[None], summed_grad * norm_factor)


def solution(mesh):
    placed = (
        P("dp", "seq", None),
        P("seq", None),
        P("seq", None),
        P("dp", None, "seq"),
        P("dp", "seq", None),
    )
    return jax.shard_map(
        local,
        mesh=mesh,
        in_specs=placed,
        out_specs=(P("dp", "seq", None), P("seq", None)),
        check_vma=False,
    )
```

```python
import math

import jax
import jax.numpy as jnp
from jax import lax
from jax.sharding import PartitionSpec as P
from jax.experimental import pallas as pl
from jax.experimental.pallas import tpu as pltpu


def shifted(value, axis, step, reverse):
    count = lax.axis_size(axis)
    if reverse:
        pairs = [(place, place - step) for place in range(step, count)]
    else:
        pairs = [(place, place + step) for place in range(count - step)]
    return lax.ppermute(value.astype(jnp.bfloat16), axis, pairs).astype(value.dtype)


def scan_entering(decay, state, axis, reverse):
    head_count = state.shape[0]
    flat = state.reshape(head_count, -1)
    split = flat.shape[1]
    count = lax.axis_size(axis)

    def send(part, step):
        flat, decay = part
        high = lax.reduce_precision(decay, exponent_bits=8, mantissa_bits=7)
        lanes = lambda piece: jnp.broadcast_to(piece[:, None], (head_count, 128))
        packed = jnp.concatenate([flat, lanes(high), lanes(decay - high)], axis=1)
        got = shifted(packed, axis, step, reverse)
        return got[:, :split], got[:, split] + got[:, split + 128]

    def chain(parts):
        flat, decay = parts[0]
        for later_flat, later_decay in parts[1:]:
            flat = later_decay[:, None] * flat + later_flat
            decay = decay * later_decay
        return flat, decay

    radix = 2
    own = (flat, decay)
    part = chain([send(own, step) for step in range(radix, 0, -1)])
    width = radix
    while width < count:
        pieces = min(radix, -(-count // width))
        part = chain([send(part, width * m) for m in range(pieces - 1, 0, -1)] + [part])
        width *= pieces
    flat = part[0]
    return flat.reshape(state.shape)


def butterfly_sum(value, axis):
    count = lax.axis_size(axis)
    step = 1
    while step < count:
        pairs = [(place, place ^ step) for place in range(count)]
        value = value + lax.ppermute(value, axis, pairs)
        step *= 2
    return value


def digit_reduce(value, axis, where, stride, radix):
    count = lax.axis_size(axis)
    digit = (lax.axis_index(axis) // stride) % radix
    total = lax.dynamic_index_in_dim(value, digit, where, False).astype(jnp.float32)
    for offset in range(1, radix):
        piece = lax.dynamic_index_in_dim(value, (digit + offset) % radix, where, False)
        pairs = [
            (place, place + (((place // stride) % radix + offset) % radix - (place // stride) % radix) * stride)
            for place in range(count)
        ]
        got = lax.ppermute(piece.astype(jnp.bfloat16), axis, pairs)
        total = total + got.astype(jnp.float32)
    return total


def seq_reduce_scatter(partial, axis):
    rows, cols = partial.shape
    count = lax.axis_size(axis)
    block = rows // count
    value = partial.reshape(count // 8, 4, 2, block, cols)
    value = digit_reduce(value, axis, 2, 1, 2)
    half = cols // 2
    first = digit_reduce(value[..., :half], axis, 1, 2, 4)
    first = digit_reduce(first, axis, 0, 8, count // 8)
    second = digit_reduce(value[..., half:], axis, 0, 8, count // 8)
    second = digit_reduce(second, axis, 0, 2, 4)
    return jnp.concatenate([first, second], axis=1)


def replicated_sum(value, axis):
    count = lax.axis_size(axis)
    me = lax.axis_index(axis)
    slabs = value.reshape(count, value.shape[0] // count, value.shape[1])
    total = lax.dynamic_index_in_dim(slabs, me, 0, False)
    for offset in range(1, count):
        piece = lax.dynamic_index_in_dim(slabs, (me + offset) % count, 0, False)
        pairs = [(place, (place + offset) % count) for place in range(count)]
        total = total + lax.ppermute(piece, axis, pairs)
    gathered = [total]
    for offset in range(1, count):
        pairs = [(place, (place + offset) % count) for place in range(count)]
        gathered.append(lax.ppermute(total, axis, pairs))
    stacked = jnp.stack(gathered)
    order = (me - jnp.arange(count)) % count
    return jnp.take(stacked, order, axis=0).reshape(value.shape)


def outer_kernel(left_ref, right_ref, out_ref):
    out_ref[...] = jnp.dot(
        left_ref[...], right_ref[...], preferred_element_type=jnp.float32
    ).astype(out_ref.dtype)


def outer_product(left, right):
    depth, rows = left.shape
    cols = right.shape[1]
    tile = 2048
    return pl.pallas_call(
        outer_kernel,
        grid=(rows // tile,),
        in_specs=[
            pl.BlockSpec((tile, depth), lambda i: (i, 0)),
            pl.BlockSpec((depth, cols), lambda i: (0, 0)),
        ],
        out_specs=pl.BlockSpec((tile, cols), lambda i: (i, 0)),
        out_shape=jax.ShapeDtypeStruct((rows, cols), jnp.bfloat16),
        cost_estimate=pl.CostEstimate(
            flops=2 * depth * rows * cols,
            bytes_accessed=2 * (depth * rows + depth * cols + rows * cols),
            transcendentals=0,
        ),
    )(left.T, right)


def dequantize(code_rows, scale_rows):
    row_count, col_count = code_rows.shape
    group_count = scale_rows.shape[1]
    spread = code_rows.astype(jnp.float32).reshape(row_count, group_count, col_count // group_count)
    spread = spread * scale_rows.astype(jnp.float32)[:, :, None]
    return spread.reshape(row_count, col_count).astype(jnp.bfloat16)


def block_prep(ld_block):
    cum_log = jnp.cumsum(ld_block, axis=1)
    input_scale = jnp.sqrt(-jnp.expm1(2.0 * ld_block))
    tail_weight = jnp.exp(cum_log[:, -1:] - cum_log) * input_scale
    return (cum_log, input_scale, tail_weight)


def weighted_pair(x_vals, grad_out, tail_weight, cum_log, inv_root):
    head_weight = jnp.exp(cum_log) * inv_root
    weighted_x = (x_vals.astype(jnp.float32) * tail_weight.T[:, :, None]).astype(jnp.bfloat16)
    weighted_g = (grad_out.astype(jnp.float32) * head_weight.T[:, :, None]).astype(jnp.bfloat16)
    return (weighted_x, weighted_g)


def summaries(x_vals, b_mat, c_mat, grad_out, ld_block):
    cum_log, input_scale, tail_weight = block_prep(ld_block)
    inv_root = 1.0 / math.sqrt(b_mat.shape[1])
    weighted_x, weighted_g = weighted_pair(x_vals, grad_out, tail_weight, cum_log, inv_root)
    fwd_state = jnp.einsum("sn,shp->hnp", b_mat, weighted_x, preferred_element_type=jnp.float32)
    back_state = jnp.einsum("tn,thp->hnp", c_mat, weighted_g, preferred_element_type=jnp.float32)
    return (jnp.exp(cum_log[:, -1]), fwd_state, back_state)


def block_grads(x_vals, b_mat, c_mat, grad_out, ld_block, state_in, back_in):
    block_len = ld_block.shape[1]
    cum_log, input_scale, tail_weight = block_prep(ld_block)
    inv_root = 1.0 / math.sqrt(b_mat.shape[1])
    weighted_x, weighted_g = weighted_pair(x_vals, grad_out, tail_weight, cum_log, inv_root)
    row_ids = lax.broadcasted_iota(jnp.int32, (block_len, block_len), 0)
    col_ids = lax.broadcasted_iota(jnp.int32, (block_len, block_len), 1)
    lower_mask = (row_ids >= col_ids)[None]
    log_gap = cum_log[:, :, None] - cum_log[:, None, :]
    decay_mat = jnp.where(lower_mask, jnp.exp(jnp.where(lower_mask, log_gap, 0.0)), 0.0)
    state_low = state_in.astype(jnp.bfloat16)
    back_low = back_in.astype(jnp.bfloat16)
    x_dot_g = jnp.einsum("thp,shp->hts", grad_out, x_vals, preferred_element_type=jnp.float32)
    c_dot_b = jnp.dot(c_mat, b_mat.T, preferred_element_type=jnp.float32)
    mix_weights = (
        jnp.sum(decay_mat * input_scale[:, None, :] * x_dot_g, axis=0) * inv_root
    ).astype(jnp.bfloat16)
    d_c = jnp.einsum("hnp,thp->tn", state_low, weighted_g, preferred_element_type=jnp.float32)
    d_c = d_c + jnp.dot(mix_weights, b_mat, preferred_element_type=jnp.float32)
    d_b = jnp.einsum("hnp,thp->tn", back_low, weighted_x, preferred_element_type=jnp.float32)
    d_b = d_b + jnp.dot(mix_weights.T, c_mat, preferred_element_type=jnp.float32)
    d_x = (
        jnp.einsum("tn,hnp->thp", b_mat, back_low, preferred_element_type=jnp.float32)
        * tail_weight.T[:, :, None]
    )
    inner_weights = (decay_mat * c_dot_b[None] * inv_root).astype(jnp.bfloat16)
    inner = jnp.einsum("hus,uhp->shp", inner_weights, grad_out, preferred_element_type=jnp.float32)
    d_x = d_x + input_scale.T[:, :, None] * inner
    return (d_x, d_b, d_c)


def state_chain(decays, adds, start, backward):

    def step(carry, item):
        return (item[0][:, None, None] * carry + item[1], carry)

    return lax.scan(step, start, (decays, adds), reverse=backward)


def local(inputs, weight_codes, scales, log_decay, cotangent):
    tok_count = inputs.shape[1]
    features = inputs[0]
    grad_out = cotangent[0]
    head_count = log_decay.shape[1]
    hp_width = grad_out.shape[1]
    head_dim = hp_width // head_count
    proj_width = weight_codes.shape[1]
    state_width = (proj_width - hp_width) // 2
    weights = lax.all_gather(dequantize(weight_codes, scales), "seq", axis=0, tiled=True)
    projected = jnp.dot(features, weights, preferred_element_type=jnp.float32).astype(jnp.bfloat16)
    block_len = min(128, tok_count)
    block_count = tok_count // block_len
    x_blocks = projected[:, :hp_width].reshape(block_count, block_len, head_count, head_dim)
    b_blocks = projected[:, hp_width : hp_width + state_width].reshape(
        block_count, block_len, state_width
    )
    c_blocks = projected[:, hp_width + state_width :].reshape(block_count, block_len, state_width)
    g_blocks = grad_out.reshape(block_count, block_len, head_count, head_dim)
    ld_blocks = log_decay[0].reshape(head_count, block_count, block_len).transpose(1, 0, 2)
    decays, fwd_states, back_states = jax.vmap(summaries)(
        x_blocks, b_blocks, c_blocks, g_blocks, ld_blocks
    )
    zero_state = jnp.zeros((head_count, state_width, head_dim), jnp.float32)
    dev_decay = jnp.prod(decays, axis=0)
    dev_fwd, unused_a = state_chain(decays, fwd_states, zero_state, False)
    dev_back, unused_b = state_chain(decays, back_states, zero_state, True)
    carried = (None, scan_entering(dev_decay, dev_fwd, "seq", False))
    returned = (None, scan_entering(dev_decay, dev_back, "seq", True))
    unused_c, state_starts = state_chain(decays, fwd_states, carried[1], False)
    unused_d, back_starts = state_chain(decays, back_states, returned[1], True)
    d_x, d_b, d_c = lax.map(
        lambda block_item: block_grads(*block_item),
        (x_blocks, b_blocks, c_blocks, g_blocks, ld_blocks, state_starts, back_starts),
    )
    d_proj = jnp.concatenate(
        [
            d_x.reshape(tok_count, hp_width),
            d_b.reshape(tok_count, state_width),
            d_c.reshape(tok_count, state_width),
        ],
        axis=1,
    ).astype(jnp.bfloat16)
    grad_in = lax.dot_general(
        d_proj, weights, (((1,), (1,)), ((), ())), preferred_element_type=jnp.float32
    )
    seq_count = lax.axis_size("seq")
    group_count = lax.axis_size("dp")
    norm_factor = 1.0 / math.sqrt(group_count * seq_count * tok_count)
    partial_grad = seq_reduce_scatter(
        outer_product(features, d_proj),
        "seq",
    )
    summed_grad = replicated_sum(partial_grad, "dp")
    return (grad_in[None], summed_grad * norm_factor)


def solution(mesh):
    placed = (
        P("dp", "seq", None),
        P("seq", None),
        P("seq", None),
        P("dp", None, "seq"),
        P("dp", "seq", None),
    )
    return jax.shard_map(
        local,
        mesh=mesh,
        in_specs=placed,
        out_specs=(P("dp", "seq", None), P("seq", None)),
        check_vma=False,
    )
```

```python
import math

import jax
import jax.numpy as jnp
from jax import lax
from jax.sharding import PartitionSpec as P
from jax.experimental import pallas as pl
from jax.experimental.pallas import tpu as pltpu


def shifted(value, axis, step, reverse):
    count = lax.axis_size(axis)
    if reverse:
        pairs = [(place, place - step) for place in range(step, count)]
    else:
        pairs = [(place, place + step) for place in range(count - step)]
    return lax.ppermute(value.astype(jnp.bfloat16), axis, pairs).astype(value.dtype)


def scan_entering(decay, state, axis, reverse):
    head_count = state.shape[0]
    flat = state.reshape(head_count, -1)
    split = flat.shape[1]
    count = lax.axis_size(axis)

    def send(part, step):
        flat, decay = part
        high = lax.reduce_precision(decay, exponent_bits=8, mantissa_bits=7)
        lanes = lambda piece: jnp.broadcast_to(piece[:, None], (head_count, 128))
        packed = jnp.concatenate([flat, lanes(high), lanes(decay - high)], axis=1)
        got = shifted(packed, axis, step, reverse)
        return got[:, :split], got[:, split] + got[:, split + 128]

    def chain(parts):
        flat, decay = parts[0]
        for later_flat, later_decay in parts[1:]:
            flat = later_decay[:, None] * flat + later_flat
            decay = decay * later_decay
        return flat, decay

    radix = 2
    own = (flat, decay)
    part = chain([send(own, step) for step in range(radix, 0, -1)])
    width = radix
    while width < count:
        pieces = min(radix, -(-count // width))
        part = chain([send(part, width * m) for m in range(pieces - 1, 0, -1)] + [part])
        width *= pieces
    flat = part[0]
    return flat.reshape(state.shape)


def butterfly_sum(value, axis):
    count = lax.axis_size(axis)
    step = 1
    while step < count:
        pairs = [(place, place ^ step) for place in range(count)]
        value = value + lax.ppermute(value, axis, pairs)
        step *= 2
    return value


def digit_reduce(value, axis, where, stride, radix):
    count = lax.axis_size(axis)
    digit = (lax.axis_index(axis) // stride) % radix
    total = lax.dynamic_index_in_dim(value, digit, where, False).astype(jnp.float32)
    low = value.astype(jnp.bfloat16)
    for offset in range(1, radix):
        piece = lax.dynamic_index_in_dim(low, (digit + offset) % radix, where, False)
        pairs = [
            (place, place + (((place // stride) % radix + offset) % radix - (place // stride) % radix) * stride)
            for place in range(count)
        ]
        got = lax.ppermute(piece.astype(jnp.bfloat16), axis, pairs)
        total = total + got.astype(jnp.float32)
    return total


def seq_reduce_scatter(partial, axis):
    rows, cols = partial.shape
    count = lax.axis_size(axis)
    block = rows // count
    value = partial.reshape(count // 8, 4, 2, block, cols)
    value = digit_reduce(value, axis, 2, 1, 2)
    half = cols // 2
    first = digit_reduce(value[..., :half], axis, 1, 2, 4)
    first = digit_reduce(first, axis, 0, 8, count // 8)
    second = digit_reduce(value[..., half:], axis, 0, 8, count // 8)
    second = digit_reduce(second, axis, 0, 2, 4)
    return jnp.concatenate([first, second], axis=1)


def replicated_sum(value, axis):
    count = lax.axis_size(axis)
    me = lax.axis_index(axis)
    slabs = value.reshape(count, value.shape[0] // count, value.shape[1])
    total = lax.dynamic_index_in_dim(slabs, me, 0, False)
    for offset in range(1, count):
        piece = lax.dynamic_index_in_dim(slabs, (me + offset) % count, 0, False)
        pairs = [(place, (place + offset) % count) for place in range(count)]
        total = total + lax.ppermute(piece, axis, pairs)
    gathered = [total]
    for offset in range(1, count):
        pairs = [(place, (place + offset) % count) for place in range(count)]
        gathered.append(lax.ppermute(total, axis, pairs))
    stacked = jnp.stack(gathered)
    order = (me - jnp.arange(count)) % count
    return jnp.take(stacked, order, axis=0).reshape(value.shape)


def outer_kernel(left_ref, right_ref, out_ref):
    out_ref[...] = jnp.dot(
        left_ref[...], right_ref[...], preferred_element_type=jnp.float32
    ).astype(out_ref.dtype)


def outer_product(left, right):
    depth, rows = left.shape
    cols = right.shape[1]
    tile = 2048
    return pl.pallas_call(
        outer_kernel,
        grid=(rows // tile,),
        in_specs=[
            pl.BlockSpec((tile, depth), lambda i: (i, 0)),
            pl.BlockSpec((depth, cols), lambda i: (0, 0)),
        ],
        out_specs=pl.BlockSpec((tile, cols), lambda i: (i, 0)),
        out_shape=jax.ShapeDtypeStruct((rows, cols), jnp.bfloat16),
        cost_estimate=pl.CostEstimate(
            flops=2 * depth * rows * cols,
            bytes_accessed=2 * (depth * rows + depth * cols + rows * cols),
            transcendentals=0,
        ),
    )(left.T, right)


def dequantize(code_rows, scale_rows):
    row_count, col_count = code_rows.shape
    group_count = scale_rows.shape[1]
    spread = code_rows.astype(jnp.float32).reshape(row_count, group_count, col_count // group_count)
    spread = spread * scale_rows.astype(jnp.float32)[:, :, None]
    return spread.reshape(row_count, col_count).astype(jnp.bfloat16)


def block_prep(ld_block):
    cum_log = jnp.cumsum(ld_block, axis=1)
    input_scale = jnp.sqrt(-jnp.expm1(2.0 * ld_block))
    tail_weight = jnp.exp(cum_log[:, -1:] - cum_log) * input_scale
    return (cum_log, input_scale, tail_weight)


def weighted_pair(x_vals, grad_out, tail_weight, cum_log, inv_root):
    head_weight = jnp.exp(cum_log) * inv_root
    weighted_x = (x_vals.astype(jnp.float32) * tail_weight.T[:, :, None]).astype(jnp.bfloat16)
    weighted_g = (grad_out.astype(jnp.float32) * head_weight.T[:, :, None]).astype(jnp.bfloat16)
    return (weighted_x, weighted_g)


def summaries(x_vals, b_mat, c_mat, grad_out, ld_block):
    cum_log, input_scale, tail_weight = block_prep(ld_block)
    inv_root = 1.0 / math.sqrt(b_mat.shape[1])
    weighted_x, weighted_g = weighted_pair(x_vals, grad_out, tail_weight, cum_log, inv_root)
    fwd_state = jnp.einsum("sn,shp->hnp", b_mat, weighted_x, preferred_element_type=jnp.float32)
    back_state = jnp.einsum("tn,thp->hnp", c_mat, weighted_g, preferred_element_type=jnp.float32)
    return (jnp.exp(cum_log[:, -1]), fwd_state, back_state)


def block_grads(x_vals, b_mat, c_mat, grad_out, ld_block, state_in, back_in):
    block_len = ld_block.shape[1]
    cum_log, input_scale, tail_weight = block_prep(ld_block)
    inv_root = 1.0 / math.sqrt(b_mat.shape[1])
    weighted_x, weighted_g = weighted_pair(x_vals, grad_out, tail_weight, cum_log, inv_root)
    row_ids = lax.broadcasted_iota(jnp.int32, (block_len, block_len), 0)
    col_ids = lax.broadcasted_iota(jnp.int32, (block_len, block_len), 1)
    lower_mask = (row_ids >= col_ids)[None]
    log_gap = cum_log[:, :, None] - cum_log[:, None, :]
    decay_mat = jnp.where(lower_mask, jnp.exp(jnp.where(lower_mask, log_gap, 0.0)), 0.0)
    state_low = state_in.astype(jnp.bfloat16)
    back_low = back_in.astype(jnp.bfloat16)
    x_dot_g = jnp.einsum("thp,shp->hts", grad_out, x_vals, preferred_element_type=jnp.float32)
    c_dot_b = jnp.dot(c_mat, b_mat.T, preferred_element_type=jnp.float32)
    mix_weights = (
        jnp.sum(decay_mat * input_scale[:, None, :] * x_dot_g, axis=0) * inv_root
    ).astype(jnp.bfloat16)
    d_c = jnp.einsum("hnp,thp->tn", state_low, weighted_g, preferred_element_type=jnp.float32)
    d_c = d_c + jnp.dot(mix_weights, b_mat, preferred_element_type=jnp.float32)
    d_b = jnp.einsum("hnp,thp->tn", back_low, weighted_x, preferred_element_type=jnp.float32)
    d_b = d_b + jnp.dot(mix_weights.T, c_mat, preferred_element_type=jnp.float32)
    d_x = (
        jnp.einsum("tn,hnp->thp", b_mat, back_low, preferred_element_type=jnp.float32)
        * tail_weight.T[:, :, None]
    )
    inner_weights = (decay_mat * c_dot_b[None] * inv_root).astype(jnp.bfloat16)
    inner = jnp.einsum("hus,uhp->shp", inner_weights, grad_out, preferred_element_type=jnp.float32)
    d_x = d_x + input_scale.T[:, :, None] * inner
    return (d_x, d_b, d_c)


def state_chain(decays, adds, start, backward):

    def step(carry, item):
        return (item[0][:, None, None] * carry + item[1], carry)

    return lax.scan(step, start, (decays, adds), reverse=backward)


def local(inputs, weight_codes, scales, log_decay, cotangent):
    tok_count = inputs.shape[1]
    features = inputs[0]
    grad_out = cotangent[0]
    head_count = log_decay.shape[1]
    hp_width = grad_out.shape[1]
    head_dim = hp_width // head_count
    proj_width = weight_codes.shape[1]
    state_width = (proj_width - hp_width) // 2
    weights = lax.all_gather(dequantize(weight_codes, scales), "seq", axis=0, tiled=True)
    projected = jnp.dot(features, weights, preferred_element_type=jnp.float32).astype(jnp.bfloat16)
    block_len = min(128, tok_count)
    block_count = tok_count // block_len
    x_blocks = projected[:, :hp_width].reshape(block_count, block_len, head_count, head_dim)
    b_blocks = projected[:, hp_width : hp_width + state_width].reshape(
        block_count, block_len, state_width
    )
    c_blocks = projected[:, hp_width + state_width :].reshape(block_count, block_len, state_width)
    g_blocks = grad_out.reshape(block_count, block_len, head_count, head_dim)
    ld_blocks = log_decay[0].reshape(head_count, block_count, block_len).transpose(1, 0, 2)
    decays, fwd_states, back_states = jax.vmap(summaries)(
        x_blocks, b_blocks, c_blocks, g_blocks, ld_blocks
    )
    zero_state = jnp.zeros((head_count, state_width, head_dim), jnp.float32)
    dev_decay = jnp.prod(decays, axis=0)
    dev_fwd, unused_a = state_chain(decays, fwd_states, zero_state, False)
    dev_back, unused_b = state_chain(decays, back_states, zero_state, True)
    carried = (None, scan_entering(dev_decay, dev_fwd, "seq", False))
    returned = (None, scan_entering(dev_decay, dev_back, "seq", True))
    unused_c, state_starts = state_chain(decays, fwd_states, carried[1], False)
    unused_d, back_starts = state_chain(decays, back_states, returned[1], True)
    d_x, d_b, d_c = lax.map(
        lambda block_item: block_grads(*block_item),
        (x_blocks, b_blocks, c_blocks, g_blocks, ld_blocks, state_starts, back_starts),
    )
    d_proj = jnp.concatenate(
        [
            d_x.reshape(tok_count, hp_width),
            d_b.reshape(tok_count, state_width),
            d_c.reshape(tok_count, state_width),
        ],
        axis=1,
    ).astype(jnp.bfloat16)
    grad_in = lax.dot_general(
        d_proj, weights, (((1,), (1,)), ((), ())), preferred_element_type=jnp.float32
    )
    seq_count = lax.axis_size("seq")
    group_count = lax.axis_size("dp")
    norm_factor = 1.0 / math.sqrt(group_count * seq_count * tok_count)
    partial_grad = seq_reduce_scatter(
        outer_product(features, d_proj),
        "seq",
    )
    summed_grad = replicated_sum(partial_grad, "dp")
    return (grad_in[None], summed_grad * norm_factor)


def solution(mesh):
    placed = (
        P("dp", "seq", None),
        P("seq", None),
        P("seq", None),
        P("dp", None, "seq"),
        P("dp", "seq", None),
    )
    return jax.shard_map(
        local,
        mesh=mesh,
        in_specs=placed,
        out_specs=(P("dp", "seq", None), P("seq", None)),
        check_vma=False,
    )
```

```python
import math

import jax
import jax.numpy as jnp
from jax import lax
from jax.sharding import PartitionSpec as P
from jax.experimental import pallas as pl
from jax.experimental.pallas import tpu as pltpu


def shifted(value, axis, step, reverse):
    count = lax.axis_size(axis)
    if reverse:
        pairs = [(place, place - step) for place in range(step, count)]
    else:
        pairs = [(place, place + step) for place in range(count - step)]
    return lax.ppermute(value.astype(jnp.bfloat16), axis, pairs).astype(value.dtype)


def scan_entering(decay, state, axis, reverse):
    head_count = state.shape[0]
    flat = state.reshape(head_count, -1)
    split = flat.shape[1]
    count = lax.axis_size(axis)

    def send(part, step):
        flat, decay = part
        high = lax.reduce_precision(decay, exponent_bits=8, mantissa_bits=7)
        lanes = lambda piece: jnp.broadcast_to(piece[:, None], (head_count, 128))
        packed = jnp.concatenate([flat, lanes(high), lanes(decay - high)], axis=1)
        got = shifted(packed, axis, step, reverse)
        return got[:, :split], got[:, split] + got[:, split + 128]

    def chain(parts):
        flat, decay = parts[0]
        for later_flat, later_decay in parts[1:]:
            flat = later_decay[:, None] * flat + later_flat
            decay = decay * later_decay
        return flat, decay

    radix = 2
    own = (flat, decay)
    part = chain([send(own, step) for step in range(radix, 0, -1)])
    width = radix
    while width < count:
        pieces = min(radix, -(-count // width))
        part = chain([send(part, width * m) for m in range(pieces - 1, 0, -1)] + [part])
        width *= pieces
    flat = part[0]
    return flat.reshape(state.shape)


def butterfly_sum(value, axis):
    count = lax.axis_size(axis)
    step = 1
    while step < count:
        pairs = [(place, place ^ step) for place in range(count)]
        value = value + lax.ppermute(value, axis, pairs)
        step *= 2
    return value


def digit_reduce(value, axis, where, stride, radix):
    count = lax.axis_size(axis)
    digit = (lax.axis_index(axis) // stride) % radix
    total = lax.dynamic_index_in_dim(value, digit, where, False).astype(jnp.float32)
    low = value.astype(jnp.bfloat16)
    for offset in sorted(range(1, radix), key=lambda o: -min(o, radix - o)):
        piece = lax.dynamic_index_in_dim(low, (digit + offset) % radix, where, False)
        pairs = [
            (place, place + (((place // stride) % radix + offset) % radix - (place // stride) % radix) * stride)
            for place in range(count)
        ]
        got = lax.ppermute(piece.astype(jnp.bfloat16), axis, pairs)
        total = total + got.astype(jnp.float32)
    return total


def seq_reduce_scatter(partial, axis):
    rows, cols = partial.shape
    count = lax.axis_size(axis)
    block = rows // count
    value = partial.reshape(count // 8, 4, 2, block, cols)
    value = digit_reduce(value, axis, 2, 1, 2)
    half = cols // 2
    first = digit_reduce(value[..., :half], axis, 1, 2, 4)
    first = digit_reduce(first, axis, 0, 8, count // 8)
    second = digit_reduce(value[..., half:], axis, 0, 8, count // 8)
    second = digit_reduce(second, axis, 0, 2, 4)
    return jnp.concatenate([first, second], axis=1)


def replicated_sum(value, axis):
    count = lax.axis_size(axis)
    me = lax.axis_index(axis)
    slabs = value.reshape(count, value.shape[0] // count, value.shape[1])
    total = lax.dynamic_index_in_dim(slabs, me, 0, False)
    for offset in range(1, count):
        piece = lax.dynamic_index_in_dim(slabs, (me + offset) % count, 0, False)
        pairs = [(place, (place + offset) % count) for place in range(count)]
        total = total + lax.ppermute(piece, axis, pairs)
    gathered = [total]
    for offset in range(1, count):
        pairs = [(place, (place + offset) % count) for place in range(count)]
        gathered.append(lax.ppermute(total, axis, pairs))
    stacked = jnp.stack(gathered)
    order = (me - jnp.arange(count)) % count
    return jnp.take(stacked, order, axis=0).reshape(value.shape)


def outer_kernel(left_ref, right_ref, out_ref):
    out_ref[...] = jnp.dot(
        left_ref[...], right_ref[...], preferred_element_type=jnp.float32
    ).astype(out_ref.dtype)


def outer_product(left, right):
    depth, rows = left.shape
    cols = right.shape[1]
    tile = 2048
    return pl.pallas_call(
        outer_kernel,
        grid=(rows // tile,),
        in_specs=[
            pl.BlockSpec((tile, depth), lambda i: (i, 0)),
            pl.BlockSpec((depth, cols), lambda i: (0, 0)),
        ],
        out_specs=pl.BlockSpec((tile, cols), lambda i: (i, 0)),
        out_shape=jax.ShapeDtypeStruct((rows, cols), jnp.bfloat16),
        cost_estimate=pl.CostEstimate(
            flops=2 * depth * rows * cols,
            bytes_accessed=2 * (depth * rows + depth * cols + rows * cols),
            transcendentals=0,
        ),
    )(left.T, right)


def dequantize(code_rows, scale_rows):
    row_count, col_count = code_rows.shape
    group_count = scale_rows.shape[1]
    spread = code_rows.astype(jnp.float32).reshape(row_count, group_count, col_count // group_count)
    spread = spread * scale_rows.astype(jnp.float32)[:, :, None]
    return spread.reshape(row_count, col_count).astype(jnp.bfloat16)


def block_prep(ld_block):
    cum_log = jnp.cumsum(ld_block, axis=1)
    input_scale = jnp.sqrt(-jnp.expm1(2.0 * ld_block))
    tail_weight = jnp.exp(cum_log[:, -1:] - cum_log) * input_scale
    return (cum_log, input_scale, tail_weight)


def weighted_pair(x_vals, grad_out, tail_weight, cum_log, inv_root):
    head_weight = jnp.exp(cum_log) * inv_root
    weighted_x = (x_vals.astype(jnp.float32) * tail_weight.T[:, :, None]).astype(jnp.bfloat16)
    weighted_g = (grad_out.astype(jnp.float32) * head_weight.T[:, :, None]).astype(jnp.bfloat16)
    return (weighted_x, weighted_g)


def summaries(x_vals, b_mat, c_mat, grad_out, ld_block):
    cum_log, input_scale, tail_weight = block_prep(ld_block)
    inv_root = 1.0 / math.sqrt(b_mat.shape[1])
    weighted_x, weighted_g = weighted_pair(x_vals, grad_out, tail_weight, cum_log, inv_root)
    fwd_state = jnp.einsum("sn,shp->hnp", b_mat, weighted_x, preferred_element_type=jnp.float32)
    back_state = jnp.einsum("tn,thp->hnp", c_mat, weighted_g, preferred_element_type=jnp.float32)
    return (jnp.exp(cum_log[:, -1]), fwd_state, back_state)


def block_grads(x_vals, b_mat, c_mat, grad_out, ld_block, state_in, back_in):
    block_len = ld_block.shape[1]
    cum_log, input_scale, tail_weight = block_prep(ld_block)
    inv_root = 1.0 / math.sqrt(b_mat.shape[1])
    weighted_x, weighted_g = weighted_pair(x_vals, grad_out, tail_weight, cum_log, inv_root)
    row_ids = lax.broadcasted_iota(jnp.int32, (block_len, block_len), 0)
    col_ids = lax.broadcasted_iota(jnp.int32, (block_len, block_len), 1)
    lower_mask = (row_ids >= col_ids)[None]
    log_gap = cum_log[:, :, None] - cum_log[:, None, :]
    decay_mat = jnp.where(lower_mask, jnp.exp(jnp.where(lower_mask, log_gap, 0.0)), 0.0)
    state_low = state_in.astype(jnp.bfloat16)
    back_low = back_in.astype(jnp.bfloat16)
    x_dot_g = jnp.einsum("thp,shp->hts", grad_out, x_vals, preferred_element_type=jnp.float32)
    c_dot_b = jnp.dot(c_mat, b_mat.T, preferred_element_type=jnp.float32)
    mix_weights = (
        jnp.sum(decay_mat * input_scale[:, None, :] * x_dot_g, axis=0) * inv_root
    ).astype(jnp.bfloat16)
    d_c = jnp.einsum("hnp,thp->tn", state_low, weighted_g, preferred_element_type=jnp.float32)
    d_c = d_c + jnp.dot(mix_weights, b_mat, preferred_element_type=jnp.float32)
    d_b = jnp.einsum("hnp,thp->tn", back_low, weighted_x, preferred_element_type=jnp.float32)
    d_b = d_b + jnp.dot(mix_weights.T, c_mat, preferred_element_type=jnp.float32)
    d_x = (
        jnp.einsum("tn,hnp->thp", b_mat, back_low, preferred_element_type=jnp.float32)
        * tail_weight.T[:, :, None]
    )
    inner_weights = (decay_mat * c_dot_b[None] * inv_root).astype(jnp.bfloat16)
    inner = jnp.einsum("hus,uhp->shp", inner_weights, grad_out, preferred_element_type=jnp.float32)
    d_x = d_x + input_scale.T[:, :, None] * inner
    return (d_x, d_b, d_c)


def state_chain(decays, adds, start, backward):

    def step(carry, item):
        return (item[0][:, None, None] * carry + item[1], carry)

    return lax.scan(step, start, (decays, adds), reverse=backward)


def local(inputs, weight_codes, scales, log_decay, cotangent):
    tok_count = inputs.shape[1]
    features = inputs[0]
    grad_out = cotangent[0]
    head_count = log_decay.shape[1]
    hp_width = grad_out.shape[1]
    head_dim = hp_width // head_count
    proj_width = weight_codes.shape[1]
    state_width = (proj_width - hp_width) // 2
    weights = lax.all_gather(dequantize(weight_codes, scales), "seq", axis=0, tiled=True)
    projected = jnp.dot(features, weights, preferred_element_type=jnp.float32).astype(jnp.bfloat16)
    block_len = min(128, tok_count)
    block_count = tok_count // block_len
    x_blocks = projected[:, :hp_width].reshape(block_count, block_len, head_count, head_dim)
    b_blocks = projected[:, hp_width : hp_width + state_width].reshape(
        block_count, block_len, state_width
    )
    c_blocks = projected[:, hp_width + state_width :].reshape(block_count, block_len, state_width)
    g_blocks = grad_out.reshape(block_count, block_len, head_count, head_dim)
    ld_blocks = log_decay[0].reshape(head_count, block_count, block_len).transpose(1, 0, 2)
    decays, fwd_states, back_states = jax.vmap(summaries)(
        x_blocks, b_blocks, c_blocks, g_blocks, ld_blocks
    )
    zero_state = jnp.zeros((head_count, state_width, head_dim), jnp.float32)
    dev_decay = jnp.prod(decays, axis=0)
    dev_fwd, unused_a = state_chain(decays, fwd_states, zero_state, False)
    dev_back, unused_b = state_chain(decays, back_states, zero_state, True)
    carried = (None, scan_entering(dev_decay, dev_fwd, "seq", False))
    returned = (None, scan_entering(dev_decay, dev_back, "seq", True))
    unused_c, state_starts = state_chain(decays, fwd_states, carried[1], False)
    unused_d, back_starts = state_chain(decays, back_states, returned[1], True)
    d_x, d_b, d_c = lax.map(
        lambda block_item: block_grads(*block_item),
        (x_blocks, b_blocks, c_blocks, g_blocks, ld_blocks, state_starts, back_starts),
    )
    d_proj = jnp.concatenate(
        [
            d_x.reshape(tok_count, hp_width),
            d_b.reshape(tok_count, state_width),
            d_c.reshape(tok_count, state_width),
        ],
        axis=1,
    ).astype(jnp.bfloat16)
    grad_in = lax.dot_general(
        d_proj, weights, (((1,), (1,)), ((), ())), preferred_element_type=jnp.float32
    )
    seq_count = lax.axis_size("seq")
    group_count = lax.axis_size("dp")
    norm_factor = 1.0 / math.sqrt(group_count * seq_count * tok_count)
    partial_grad = seq_reduce_scatter(
        outer_product(features, d_proj),
        "seq",
    )
    summed_grad = replicated_sum(partial_grad, "dp")
    return (grad_in[None], summed_grad * norm_factor)


def solution(mesh):
    placed = (
        P("dp", "seq", None),
        P("seq", None),
        P("seq", None),
        P("dp", None, "seq"),
        P("dp", "seq", None),
    )
    return jax.shard_map(
        local,
        mesh=mesh,
        in_specs=placed,
        out_specs=(P("dp", "seq", None), P("seq", None)),
        check_vma=False,
    )
```
